32 devices in a mesh: dp: 4 (over z), space: 4 (over x, core), rep: 2 (over y).
Axes of the slice: x: 2, y: 2, z: 4, core: 2. Of those that a mesh axis runs over, the one named last changes fastest.
Arguments:
- frames: bfloat16 [6, 8, 32, 32, 512], P(None, ('dp', 'rep'), 'space'), may hold values from -6 to 6
- membrane: bfloat16 [8, 32, 32, 512], P(('dp', 'rep'), 'space'), may hold values from -6 to 6
- cotangent: bfloat16 [6, 8, 32, 32, 512], P(None, ('dp', 'rep'), 'space'), may hold values from -6 to 6
- master: float32 [4608, 512], P('dp'), may hold values from -0.09375 to 0.09375
- moment: float32 [4608, 512], P('dp'), may hold values from -4 to 4
- second: float32 [4608, 512], P('dp'), may hold values from 0.05 to 5
Outputs:
- grad_input: bfloat16 [6, 8, 32, 32, 512], P(None, ('dp', 'rep'), 'space')
- membrane_grad: float32 [8, 32, 32, 512], P(('dp', 'rep'), 'space')
- weight_grad: float32 [4608, 512], P('dp')
- new_moment: float32 [4608, 512], P('dp')
- new_second: float32 [4608, 512], P('dp')
- update: float32 [4608, 512], P('dp')
The draws below stay inside these ranges and needn't reach their ends.
All inputs are finite; a program needn't handle non-finite values.
Results may differ from the reference program's by a relative error of at most 0.003.
Values may be sent and summed in bfloat16 or wider, within the bound.
No kernel may reach another device: no remote copies, remote signals or barrier semaphores. Data moves between devices by JAX's collectives and lax.ppermute only.
A program may use at most 192 MiB of HBM per device.

```python
import math
import jax
import jax.numpy as jnp
from jax import lax

C = 512
H = 32
W = 32
TSTEPS = 6
BATCH = 8


def block_levels(rng, dims, pieces, low, high):
    def one(dim, blocks):
        heights = jax.random.uniform(jax.random.fold_in(jax.random.fold_in(rng, 6), dim), (blocks,), jnp.float32, low / len(pieces), high / len(pieces))
        return jnp.repeat(jnp.exp(heights), dims[dim] // blocks).reshape((-1,) + (1,) * (len(dims) - dim - 1))

    loudness = one(*pieces[0])
    for cut in pieces[1:]:
        loudness = loudness * one(*cut)
    return loudness


def bell_draw(key, dims, deviation, bound, split=(), dtype=jnp.bfloat16):
    entries = deviation * jax.random.normal(key, dims, jnp.float32)
    if split:
        entries = entries * block_levels(key, dims, split, -0.22, 0.18)
    return jnp.clip(entries, -bound, bound).astype(dtype)


def setup_inputs(seed: int = 0) -> dict:
    seeds = jax.random.split(jax.random.key(seed), 7)
    frames = bell_draw(seeds[0], (TSTEPS, BATCH, H, W, C), 1.0, 6.0, ((1, 8), (2, 4)))
    membrane = bell_draw(seeds[1], (BATCH, H, W, C), 1.0, 6.0, ((0, 8), (1, 4)))
    cotangent = bell_draw(seeds[2], (TSTEPS, BATCH, H, W, C), 1.0, 6.0, ((1, 8), (2, 4)))
    master = bell_draw(seeds[3], (9 * C, C), (9 * C) ** -0.5, 0.09375, ((0, 4),), jnp.float32)
    moment = bell_draw(seeds[4], (9 * C, C), 0.5, 4.0, ((0, 4),), jnp.float32)
    second = jnp.clip(jnp.exp(math.log(5.0) - 4.6051702 * jax.random.uniform(seeds[5], (9 * C, C), jnp.float32) ** block_levels(seeds[5], (9 * C, C), ((0, 4),), -0.2, 0.2)), 0.05, 5.0)
    return dict(frames=frames, membrane=membrane, cotangent=cotangent, master=master, moment=moment, second=second)


def surrogate(potential):
    return 1.0 / (1.0 + (math.pi * (potential - 1.0)) ** 2)

def offsets_list():
    return [(row_shift, col_shift) for row_shift in (-1, 0, 1) for col_shift in (-1, 0, 1)]

def sample_grads(frames_one, membrane_one, cotangent_one, weights):
    steps_count, rows, cols, chans = frames_one.shape
    voltage = membrane_one.astype(jnp.float32)
    potentials = []
    fired = []
    for position in range(steps_count):
        potential = 0.5 * voltage + frames_one[position].astype(jnp.float32)
        spikes = jnp.where(potential >= 1.0, jnp.float32(1.0), jnp.float32(0.0))
        voltage = potential - spikes
        potentials.append(potential)
        fired.append(spikes)
    potential_all = jnp.stack(potentials)
    spike_all = jnp.stack(fired).astype(jnp.bfloat16)
    widths = ((0, 0), (1, 1), (1, 1), (0, 0))
    spike_pad = jnp.pad(spike_all, widths)
    grad_pad = jnp.pad(cotangent_one, widths)
    spike_cols = jnp.concatenate([spike_pad[:, 1 + a:1 + a + rows, 1 + b:1 + b + cols] for a, b in offsets_list()], axis=-1).reshape(-1, 9 * chans)
    grad_cols = jnp.concatenate([grad_pad[:, 1 - a:1 - a + rows, 1 - b:1 - b + cols] for a, b in offsets_list()], axis=-1).reshape(-1, 9, chans)
    grad_flat = cotangent_one.reshape(-1, chans)
    weight_part = lax.dot_general(spike_cols, grad_flat, (((0,), (0,)), ((), ())), preferred_element_type=jnp.float32)
    dspikes = jnp.einsum('nkd,kcd->nc', grad_cols.astype(jnp.float32), weights.reshape(9, chans, chans).astype(jnp.float32)).reshape(steps_count, rows, cols, chans)
    carried = jnp.zeros((rows, cols, chans), jnp.float32)
    outs = [None] * steps_count
    for position in reversed(range(steps_count)):
        carried = dspikes[position] * surrogate(potential_all[position]) + 0.5 * carried
        outs[position] = (cotangent_one[position].astype(jnp.float32) + carried).astype(jnp.bfloat16)
    return (jnp.stack(outs), 0.5 * carried, weight_part)

def reference(frames, membrane, cotangent, master, moment, second):
    weights = master.astype(jnp.bfloat16)

    def per_sample(total, items):
        frames_one, membrane_one, cotangent_one = items
        grad_one, mem_one, weight_part = sample_grads(frames_one, membrane_one, cotangent_one, weights)
        return (total + weight_part, (grad_one, mem_one))
    start = jnp.zeros(master.shape, jnp.float32)
    total, (grads, membrane_grad) = lax.scan(per_sample, start, (jnp.moveaxis(frames, 1, 0), membrane, jnp.moveaxis(cotangent, 1, 0)))
    grad_input = jnp.moveaxis(grads, 0, 1)
    weight_grad = total * (1.0 / math.sqrt(TSTEPS * BATCH * H * W))
    new_moment = 0.9 * moment + 0.1 * weight_grad
    new_second = 0.95 * second + 0.05 * weight_grad * weight_grad
    update = new_moment / (jnp.sqrt(new_second) + 1e-08)
    return (grad_input, membrane_grad, weight_grad, new_moment, new_second, update)
```

```python
import math

import jax
import jax.numpy as jnp
from jax import lax
from jax.sharding import PartitionSpec as P


def extended(x, sides, width):
    for axis, dim in sides:
        peers, length = (lax.axis_size(axis), x.shape[dim])
        up = [(i, (i + 1) % peers) for i in range(peers - 1)]
        down = [(j, i) for i, j in up]
        last = lax.slice_in_dim(x, length - width, length, axis=dim)
        first = lax.slice_in_dim(x, 0, width, axis=dim)
        before = lax.ppermute(last, axis, up)
        after = lax.ppermute(first, axis, down)
        x = jnp.concatenate([before, x, after], axis=dim)
    return x


def surrogate(potential):
    return 1.0 / (1.0 + (math.pi * (potential - 1.0)) ** 2)


def offsets_list():
    return [(row_shift, col_shift) for row_shift in (-1, 0, 1) for col_shift in (-1, 0, 1)]


def on_device(frames, membrane, cotangent, master, moment, second):
    steps_count, samples, rows, cols, chans = frames.shape
    rest = ("space", "rep")
    rest_count = lax.axis_size("space") * lax.axis_size("rep")
    data_count = lax.axis_size("dp")
    shard_rows = master.shape[0]
    piece_rows = shard_rows // rest_count
    local = master.astype(jnp.bfloat16)
    piece = lax.dynamic_slice_in_dim(local, lax.axis_index(rest) * piece_rows, piece_rows, 0)
    over_dp = lax.all_gather(piece, "dp", axis=0, tiled=False)
    over_all = lax.all_gather(over_dp, rest, axis=0, tiled=False)
    weights = jnp.swapaxes(over_all, 0, 1).reshape(data_count * shard_rows, master.shape[1])
    stacked = jnp.concatenate([membrane[None], frames], axis=0)
    rimmed = extended(stacked, (("space", 2),), 1)
    voltage = rimmed[0].astype(jnp.float32)
    potentials = []
    fired = []
    for position in range(steps_count):
        potential = 0.5 * voltage + rimmed[position + 1].astype(jnp.float32)
        spikes = jnp.where(potential >= 1.0, jnp.float32(1.0), jnp.float32(0.0))
        voltage = potential - spikes
        potentials.append(potential[:, 1:-1])
        fired.append(spikes)
    potential_all = jnp.stack(potentials)
    spike_all = jnp.stack(fired).astype(jnp.bfloat16)
    col_pad = ((0, 0), (0, 0), (0, 0), (1, 1), (0, 0))
    spike_pad = jnp.pad(spike_all, col_pad)
    grad_rim = extended(cotangent, (("space", 2),), 1)
    grad_pad = jnp.pad(grad_rim, col_pad)
    spike_cols = jnp.concatenate(
        [spike_pad[:, :, 1 + a : 1 + a + rows, 1 + b : 1 + b + cols] for a, b in offsets_list()],
        axis=-1,
    ).reshape(-1, 9 * chans)
    grad_cols = jnp.concatenate(
        [grad_pad[:, :, 1 - a : 1 - a + rows, 1 - b : 1 - b + cols] for a, b in offsets_list()],
        axis=-1,
    ).reshape(-1, 9, chans)
    grad_flat = cotangent.reshape(-1, chans)
    weight_local = lax.dot_general(
        spike_cols, grad_flat, (((0,), (0,)), ((), ())), preferred_element_type=jnp.float32
    )
    dspikes = jnp.einsum(
        "nkd,kcd->nc",
        grad_cols,
        weights.reshape(9, chans, chans),
        preferred_element_type=jnp.float32,
    )
    dspikes = dspikes.reshape(steps_count, samples, rows, cols, chans)
    carried = jnp.zeros((samples, rows, cols, chans), jnp.float32)
    outs = [None] * steps_count
    for position in reversed(range(steps_count)):
        carried = dspikes[position] * surrogate(potential_all[position]) + 0.5 * carried
        outs[position] = (cotangent[position].astype(jnp.float32) + carried).astype(jnp.bfloat16)
    grad_input = jnp.stack(outs)
    membrane_grad = 0.5 * carried
    total_cells = samples * data_count * lax.axis_size("rep") * rows * lax.axis_size("space") * cols
    shard_part = lax.psum_scatter(weight_local, ("dp",) + rest, scatter_dimension=0, tiled=True)
    summed = lax.all_gather(shard_part, rest, axis=0, tiled=True)
    weight_grad = summed * (1.0 / math.sqrt(steps_count * total_cells))
    new_moment = 0.9 * moment + 0.1 * weight_grad
    new_second = 0.95 * second + 0.05 * weight_grad * weight_grad
    update = new_moment / (jnp.sqrt(new_second) + 1e-08)
    return (grad_input, membrane_grad, weight_grad, new_moment, new_second, update)


def solution(mesh):
    return jax.shard_map(
        on_device,
        mesh=mesh,
        in_specs=(
            P(None, ("dp", "rep"), "space", None, None),
            P(("dp", "rep"), "space", None, None),
            P(None, ("dp", "rep"), "space", None, None),
            P("dp", None),
            P("dp", None),
            P("dp", None),
        ),
        out_specs=(
            P(None, ("dp", "rep"), "space", None, None),
            P(("dp", "rep"), "space", None, None),
            P("dp", None),
            P("dp", None),
            P("dp", None),
            P("dp", None),
        ),
        check_vma=False,
    )
```

```python
import math

import jax
import jax.numpy as jnp
from jax import lax
from jax.sharding import PartitionSpec as P


def extended(x, sides, width):
    for axis, dim in sides:
        peers, length = (lax.axis_size(axis), x.shape[dim])
        up = [(i, (i + 1) % peers) for i in range(peers - 1)]
        down = [(j, i) for i, j in up]
        last = lax.slice_in_dim(x, length - width, length, axis=dim)
        first = lax.slice_in_dim(x, 0, width, axis=dim)
        before = lax.ppermute(last, axis, up)
        after = lax.ppermute(first, axis, down)
        x = jnp.concatenate([before, x, after], axis=dim)
    return x


def halving_scatter(blocks, layout):
    names = list(layout)
    stage_list = sorted(layout, key=lambda e: (["space", "rep", "dp"].index(e[0]), e[1]))
    for axis, bit in stage_list:
        dim = names.index((axis, bit))
        peers = lax.axis_size(axis)
        mine = (lax.axis_index(axis) // (1 << bit)) % 2
        keep = lax.dynamic_index_in_dim(blocks, mine, dim, keepdims=False)
        send = lax.dynamic_index_in_dim(blocks, 1 - mine, dim, keepdims=False)
        pairs = [(j, j ^ (1 << bit)) for j in range(peers)]
        blocks = keep + lax.ppermute(send, axis, pairs)
        names.pop(dim)
    return blocks


def bit_count(n):
    return n.bit_length() - 1


def surrogate(potential):
    return 1.0 / (1.0 + (math.pi * (potential - 1.0)) ** 2)


def offsets_list():
    return [(row_shift, col_shift) for row_shift in (-1, 0, 1) for col_shift in (-1, 0, 1)]


def on_device(frames, membrane, cotangent, master, moment, second):
    steps_count, samples, rows, cols, chans = frames.shape
    rest = ("space", "rep")
    rest_count = lax.axis_size("space") * lax.axis_size("rep")
    data_count = lax.axis_size("dp")
    shard_rows = master.shape[0]
    piece_rows = shard_rows // rest_count
    local = master.astype(jnp.bfloat16)
    piece = lax.dynamic_slice_in_dim(local, lax.axis_index(rest) * piece_rows, piece_rows, 0)
    over_dp = lax.all_gather(piece, "dp", axis=0, tiled=False)
    over_all = lax.all_gather(over_dp, rest, axis=0, tiled=False)
    weights = jnp.swapaxes(over_all, 0, 1).reshape(data_count * shard_rows, master.shape[1])
    stacked = jnp.concatenate([membrane[None], frames], axis=0)
    rimmed = extended(stacked, (("space", 2),), 1)
    voltage = rimmed[0].astype(jnp.float32)
    potentials = []
    fired = []
    for position in range(steps_count):
        potential = 0.5 * voltage + rimmed[position + 1].astype(jnp.float32)
        spikes = jnp.where(potential >= 1.0, jnp.float32(1.0), jnp.float32(0.0))
        voltage = potential - spikes
        potentials.append(potential[:, 1:-1])
        fired.append(spikes)
    potential_all = jnp.stack(potentials)
    spike_all = jnp.stack(fired).astype(jnp.bfloat16)
    col_pad = ((0, 0), (0, 0), (0, 0), (1, 1), (0, 0))
    spike_pad = jnp.pad(spike_all, col_pad)
    grad_rim = extended(cotangent, (("space", 2),), 1)
    grad_pad = jnp.pad(grad_rim, col_pad)
    spike_cols = jnp.concatenate(
        [spike_pad[:, :, 1 + a : 1 + a + rows, 1 + b : 1 + b + cols] for a, b in offsets_list()],
        axis=-1,
    ).reshape(-1, 9 * chans)
    grad_cols = jnp.concatenate(
        [grad_pad[:, :, 1 - a : 1 - a + rows, 1 - b : 1 - b + cols] for a, b in offsets_list()],
        axis=-1,
    ).reshape(-1, 9, chans)
    grad_flat = cotangent.reshape(-1, chans)
    weight_local = lax.dot_general(
        spike_cols, grad_flat, (((0,), (0,)), ((), ())), preferred_element_type=jnp.float32
    )
    dspikes = jnp.einsum(
        "nkd,kcd->nc",
        grad_cols,
        weights.reshape(9, chans, chans),
        preferred_element_type=jnp.float32,
    )
    dspikes = dspikes.reshape(steps_count, samples, rows, cols, chans)
    carried = jnp.zeros((samples, rows, cols, chans), jnp.float32)
    outs = [None] * steps_count
    for position in reversed(range(steps_count)):
        carried = dspikes[position] * surrogate(potential_all[position]) + 0.5 * carried
        outs[position] = (cotangent[position].astype(jnp.float32) + carried).astype(jnp.bfloat16)
    grad_input = jnp.stack(outs)
    membrane_grad = 0.5 * carried
    total_cells = samples * data_count * lax.axis_size("rep") * rows * lax.axis_size("space") * cols
    layout = []
    for axis in ("dp",) + rest:
        layout += [(axis, bit) for bit in reversed(range(bit_count(lax.axis_size(axis))))]
    piece_shape = (weight_local.shape[0] // 2 ** len(layout), weight_local.shape[1])
    shard_part = halving_scatter(weight_local.reshape((2,) * len(layout) + piece_shape), layout)
    summed = lax.all_gather(shard_part, rest, axis=0, tiled=True)
    weight_grad = summed * (1.0 / math.sqrt(steps_count * total_cells))
    new_moment = 0.9 * moment + 0.1 * weight_grad
    new_second = 0.95 * second + 0.05 * weight_grad * weight_grad
    update = new_moment / (jnp.sqrt(new_second) + 1e-08)
    return (grad_input, membrane_grad, weight_grad, new_moment, new_second, update)


def solution(mesh):
    return jax.shard_map(
        on_device,
        mesh=mesh,
        in_specs=(
            P(None, ("dp", "rep"), "space", None, None),
            P(("dp", "rep"), "space", None, None),
            P(None, ("dp", "rep"), "space", None, None),
            P("dp", None),
            P("dp", None),
            P("dp", None),
        ),
        out_specs=(
            P(None, ("dp", "rep"), "space", None, None),
            P(("dp", "rep"), "space", None, None),
            P("dp", None),
            P("dp", None),
            P("dp", None),
            P("dp", None),
        ),
        check_vma=False,
    )
```

```python
import math

import jax
import jax.numpy as jnp
from jax import lax
from jax.sharding import PartitionSpec as P


def extended(x, sides, width):
    for axis, dim in sides:
        peers, length = (lax.axis_size(axis), x.shape[dim])
        up = [(i, (i + 1) % peers) for i in range(peers - 1)]
        down = [(j, i) for i, j in up]
        last = lax.slice_in_dim(x, length - width, length, axis=dim)
        first = lax.slice_in_dim(x, 0, width, axis=dim)
        before = lax.ppermute(last, axis, up)
        after = lax.ppermute(first, axis, down)
        x = jnp.concatenate([before, x, after], axis=dim)
    return x


def surrogate(potential):
    return 1.0 / (1.0 + (math.pi * (potential - 1.0)) ** 2)


def offsets_list():
    return [(row_shift, col_shift) for row_shift in (-1, 0, 1) for col_shift in (-1, 0, 1)]


def on_device(frames, membrane, cotangent, master, moment, second):
    steps_count, samples, rows, cols, chans = frames.shape
    rest = ("space", "rep")
    rest_count = lax.axis_size("space") * lax.axis_size("rep")
    data_count = lax.axis_size("dp")
    piece_rows = master.shape[0] // rest_count
    stacked = jnp.concatenate([membrane[None], frames], axis=0)
    rimmed = extended(stacked, (("space", 2),), 1)
    voltage = rimmed[0].astype(jnp.float32)
    potentials = []
    fired = []
    for position in range(steps_count):
        potential = 0.5 * voltage + rimmed[position + 1].astype(jnp.float32)
        spikes = jnp.where(potential >= 1.0, jnp.float32(1.0), jnp.float32(0.0))
        voltage = potential - spikes
        potentials.append(potential[:, 1:-1])
        fired.append(spikes)
    potential_all = jnp.stack(potentials)
    spike_all = jnp.stack(fired).astype(jnp.bfloat16)
    col_pad = ((0, 0), (0, 0), (0, 0), (1, 1), (0, 0))
    spike_pad = jnp.pad(spike_all, col_pad)
    grad_rim = extended(cotangent, (("space", 2),), 1)
    grad_pad = jnp.pad(grad_rim, col_pad)
    spike_cols = jnp.concatenate(
        [spike_pad[:, :, 1 + a : 1 + a + rows, 1 + b : 1 + b + cols] for a, b in offsets_list()],
        axis=-1,
    ).reshape(-1, 9 * chans)
    grad_cols = jnp.concatenate(
        [grad_pad[:, :, 1 - a : 1 - a + rows, 1 - b : 1 - b + cols] for a, b in offsets_list()],
        axis=-1,
    ).reshape(-1, 9, chans)
    grad_flat = cotangent.reshape(-1, chans)
    weight_local = lax.dot_general(
        spike_cols, grad_flat, (((0,), (0,)), ((), ())), preferred_element_type=jnp.float32
    )
    weight_local, local = lax.optimization_barrier((weight_local, master))
    piece = lax.dynamic_slice_in_dim(local, lax.axis_index(rest) * piece_rows, piece_rows, 0)
    weights = lax.all_gather(piece.astype(jnp.bfloat16), ("dp",) + rest, axis=0, tiled=True)
    dspikes = jnp.einsum(
        "nkd,kcd->nc",
        grad_cols,
        weights.reshape(9, chans, chans),
        preferred_element_type=jnp.float32,
    )
    dspikes = dspikes.reshape(steps_count, samples, rows, cols, chans)
    carried = jnp.zeros((samples, rows, cols, chans), jnp.float32)
    outs = [None] * steps_count
    for position in reversed(range(steps_count)):
        carried = dspikes[position] * surrogate(potential_all[position]) + 0.5 * carried
        outs[position] = (cotangent[position].astype(jnp.float32) + carried).astype(jnp.bfloat16)
    grad_input = jnp.stack(outs)
    membrane_grad = 0.5 * carried
    total_cells = samples * data_count * lax.axis_size("rep") * rows * lax.axis_size("space") * cols
    shard_part = lax.psum_scatter(weight_local, ("dp",) + rest, scatter_dimension=0, tiled=True)
    summed = lax.all_gather(shard_part, rest, axis=0, tiled=True)
    weight_grad = summed * (1.0 / math.sqrt(steps_count * total_cells))
    new_moment = 0.9 * moment + 0.1 * weight_grad
    new_second = 0.95 * second + 0.05 * weight_grad * weight_grad
    update = new_moment / (jnp.sqrt(new_second) + 1e-08)
    return (grad_input, membrane_grad, weight_grad, new_moment, new_second, update)


def solution(mesh):
    return jax.shard_map(
        on_device,
        mesh=mesh,
        in_specs=(
            P(None, ("dp", "rep"), "space", None, None),
            P(("dp", "rep"), "space", None, None),
            P(None, ("dp", "rep"), "space", None, None),
            P("dp", None),
            P("dp", None),
            P("dp", None),
        ),
        out_specs=(
            P(None, ("dp", "rep"), "space", None, None),
            P(("dp", "rep"), "space", None, None),
            P("dp", None),
            P("dp", None),
            P("dp", None),
            P("dp", None),
        ),
        check_vma=False,
    )
```

```python
import math

import jax
import jax.numpy as jnp
from jax import lax
from jax.sharding import PartitionSpec as P


def extended(x, sides, width):
    for axis, dim in sides:
        peers, length = (lax.axis_size(axis), x.shape[dim])
        up = [(i, (i + 1) % peers) for i in range(peers - 1)]
        down = [(j, i) for i, j in up]
        last = lax.slice_in_dim(x, length - width, length, axis=dim)
        first = lax.slice_in_dim(x, 0, width, axis=dim)
        before = lax.ppermute(last, axis, up)
        after = lax.ppermute(first, axis, down)
        x = jnp.concatenate([before, x, after], axis=dim)
    return x


def doubling_gather(blocks, axis):
    peers = lax.axis_size(axis)
    me = lax.axis_index(axis)
    bit = 0
    while (1 << bit) < peers:
        pairs = [(j, j ^ (1 << bit)) for j in range(peers)]
        other = lax.ppermute(blocks, axis, pairs)
        low = (me // (1 << bit)) % 2 == 0
        blocks = jnp.where(low, jnp.concatenate([blocks, other]), jnp.concatenate([other, blocks]))
        bit += 1
    return blocks


def surrogate(potential):
    return 1.0 / (1.0 + (math.pi * (potential - 1.0)) ** 2)


def offsets_list():
    return [(row_shift, col_shift) for row_shift in (-1, 0, 1) for col_shift in (-1, 0, 1)]


def on_device(frames, membrane, cotangent, master, moment, second):
    steps_count, samples, rows, cols, chans = frames.shape
    rest = ("space", "rep")
    rest_count = lax.axis_size("space") * lax.axis_size("rep")
    data_count = lax.axis_size("dp")
    shard_rows = master.shape[0]
    piece_rows = shard_rows // rest_count
    local = master.astype(jnp.bfloat16)
    piece = lax.dynamic_slice_in_dim(local, lax.axis_index(rest) * piece_rows, piece_rows, 0)
    over_dp = doubling_gather(piece[None], "dp")
    over_all = lax.all_gather(over_dp, rest, axis=0, tiled=False)
    weights = jnp.swapaxes(over_all, 0, 1).reshape(data_count * shard_rows, master.shape[1])
    stacked = jnp.concatenate([membrane[None], frames], axis=0)
    rimmed = extended(stacked, (("space", 2),), 1)
    voltage = rimmed[0].astype(jnp.float32)
    potentials = []
    fired = []
    for position in range(steps_count):
        potential = 0.5 * voltage + rimmed[position + 1].astype(jnp.float32)
        spikes = jnp.where(potential >= 1.0, jnp.float32(1.0), jnp.float32(0.0))
        voltage = potential - spikes
        potentials.append(potential[:, 1:-1])
        fired.append(spikes)
    potential_all = jnp.stack(potentials)
    spike_all = jnp.stack(fired).astype(jnp.bfloat16)
    col_pad = ((0, 0), (0, 0), (0, 0), (1, 1), (0, 0))
    spike_pad = jnp.pad(spike_all, col_pad)
    grad_rim = extended(cotangent, (("space", 2),), 1)
    grad_pad = jnp.pad(grad_rim, col_pad)
    spike_cols = jnp.concatenate(
        [spike_pad[:, :, 1 + a : 1 + a + rows, 1 + b : 1 + b + cols] for a, b in offsets_list()],
        axis=-1,
    ).reshape(-1, 9 * chans)
    grad_cols = jnp.concatenate(
        [grad_pad[:, :, 1 - a : 1 - a + rows, 1 - b : 1 - b + cols] for a, b in offsets_list()],
        axis=-1,
    ).reshape(-1, 9, chans)
    grad_flat = cotangent.reshape(-1, chans)
    weight_local = lax.dot_general(
        spike_cols, grad_flat, (((0,), (0,)), ((), ())), preferred_element_type=jnp.float32
    )
    dspikes = jnp.einsum(
        "nkd,kcd->nc",
        grad_cols,
        weights.reshape(9, chans, chans),
        preferred_element_type=jnp.float32,
    )
    dspikes = dspikes.reshape(steps_count, samples, rows, cols, chans)
    carried = jnp.zeros((samples, rows, cols, chans), jnp.float32)
    outs = [None] * steps_count
    for position in reversed(range(steps_count)):
        carried = dspikes[position] * surrogate(potential_all[position]) + 0.5 * carried
        outs[position] = (cotangent[position].astype(jnp.float32) + carried).astype(jnp.bfloat16)
    grad_input = jnp.stack(outs)
    membrane_grad = 0.5 * carried
    total_cells = samples * data_count * lax.axis_size("rep") * rows * lax.axis_size("space") * cols
    shard_part = lax.psum_scatter(weight_local, ("dp",) + rest, scatter_dimension=0, tiled=True)
    summed = lax.all_gather(shard_part, rest, axis=0, tiled=True)
    weight_grad = summed * (1.0 / math.sqrt(steps_count * total_cells))
    new_moment = 0.9 * moment + 0.1 * weight_grad
    new_second = 0.95 * second + 0.05 * weight_grad * weight_grad
    update = new_moment / (jnp.sqrt(new_second) + 1e-08)
    return (grad_input, membrane_grad, weight_grad, new_moment, new_second, update)


def solution(mesh):
    return jax.shard_map(
        on_device,
        mesh=mesh,
        in_specs=(
            P(None, ("dp", "rep"), "space", None, None),
            P(("dp", "rep"), "space", None, None),
            P(None, ("dp", "rep"), "space", None, None),
            P("dp", None),
            P("dp", None),
            P("dp", None),
        ),
        out_specs=(
            P(None, ("dp", "rep"), "space", None, None),
            P(("dp", "rep"), "space", None, None),
            P("dp", None),
            P("dp", None),
            P("dp", None),
            P("dp", None),
        ),
        check_vma=False,
    )
```

```python
import math

import jax
import jax.numpy as jnp
from jax import lax
from jax.sharding import PartitionSpec as P


def extended(x, sides, width):
    for axis, dim in sides:
        peers, length = (lax.axis_size(axis), x.shape[dim])
        up = [(i, (i + 1) % peers) for i in range(peers - 1)]
        down = [(j, i) for i, j in up]
        last = lax.slice_in_dim(x, length - width, length, axis=dim)
        first = lax.slice_in_dim(x, 0, width, axis=dim)
        before = lax.ppermute(last, axis, up)
        after = lax.ppermute(first, axis, down)
        x = jnp.concatenate([before, x, after], axis=dim)
    return x


def doubling_gather(blocks, axis):
    peers = lax.axis_size(axis)
    me = lax.axis_index(axis)
    bit = 0
    while (1 << bit) < peers:
        pairs = [(j, j ^ (1 << bit)) for j in range(peers)]
        other = lax.ppermute(blocks, axis, pairs)
        low = (me // (1 << bit)) % 2 == 0
        blocks = jnp.where(low, jnp.concatenate([blocks, other]), jnp.concatenate([other, blocks]))
        bit += 1
    return blocks


def surrogate(potential):
    return 1.0 / (1.0 + (math.pi * (potential - 1.0)) ** 2)


def offsets_list():
    return [(row_shift, col_shift) for row_shift in (-1, 0, 1) for col_shift in (-1, 0, 1)]


def on_device(frames, membrane, cotangent, master, moment, second):
    steps_count, samples, rows, cols, chans = frames.shape
    rest = ("space", "rep")
    rest_count = lax.axis_size("space") * lax.axis_size("rep")
    data_count = lax.axis_size("dp")
    shard_rows = master.shape[0]
    piece_rows = shard_rows // rest_count
    local = master.astype(jnp.bfloat16)
    piece = lax.dynamic_slice_in_dim(local, lax.axis_index(rest) * piece_rows, piece_rows, 0)
    over_dp = doubling_gather(piece[None], "dp")
    over_all = lax.all_gather(over_dp, rest, axis=0, tiled=False)
    weights = jnp.swapaxes(over_all, 0, 1).reshape(data_count * shard_rows, master.shape[1])
    stacked = jnp.concatenate([membrane[None], frames], axis=0)
    rimmed = extended(stacked, (("space", 2),), 1)
    voltage = rimmed[0].astype(jnp.float32)
    potentials = []
    fired = []
    for position in range(steps_count):
        potential = 0.5 * voltage + rimmed[position + 1].astype(jnp.float32)
        spikes = jnp.where(potential >= 1.0, jnp.float32(1.0), jnp.float32(0.0))
        voltage = potential - spikes
        potentials.append(potential[:, 1:-1])
        fired.append(spikes)
    potential_all = jnp.stack(potentials)
    spike_all = jnp.stack(fired).astype(jnp.bfloat16)
    col_pad = ((0, 0), (0, 0), (0, 0), (1, 1), (0, 0))
    spike_pad = jnp.pad(spike_all, col_pad)
    grad_rim = extended(cotangent, (("space", 2),), 1)
    grad_pad = jnp.pad(grad_rim, col_pad)
    spike_cols = jnp.concatenate(
        [spike_pad[:, :, 1 + a : 1 + a + rows, 1 + b : 1 + b + cols] for a, b in offsets_list()],
        axis=-1,
    ).reshape(-1, 9 * chans)
    grad_cols = jnp.concatenate(
        [grad_pad[:, :, 1 - a : 1 - a + rows, 1 - b : 1 - b + cols] for a, b in offsets_list()],
        axis=-1,
    ).reshape(-1, 9, chans)
    grad_flat = cotangent.reshape(-1, chans)
    half = chans // 2
    weight_halves = [
        lax.dot_general(
            spike_cols, grad_flat[:, part * half : (part + 1) * half], (((0,), (0,)), ((), ())),
            preferred_element_type=jnp.float32,
        )
        for part in range(2)
    ]
    dspikes = jnp.einsum(
        "nkd,kcd->nc",
        grad_cols,
        weights.reshape(9, chans, chans),
        preferred_element_type=jnp.float32,
    )
    dspikes = dspikes.reshape(steps_count, samples, rows, cols, chans)
    carried = jnp.zeros((samples, rows, cols, chans), jnp.float32)
    outs = [None] * steps_count
    for position in reversed(range(steps_count)):
        carried = dspikes[position] * surrogate(potential_all[position]) + 0.5 * carried
        outs[position] = (cotangent[position].astype(jnp.float32) + carried).astype(jnp.bfloat16)
    grad_input = jnp.stack(outs)
    membrane_grad = 0.5 * carried
    total_cells = samples * data_count * lax.axis_size("rep") * rows * lax.axis_size("space") * cols
    shard_part = jnp.concatenate(
        [lax.psum_scatter(part, ("dp",) + rest, scatter_dimension=0, tiled=True) for part in weight_halves], axis=1
    )
    summed = lax.all_gather(shard_part, rest, axis=0, tiled=True)
    weight_grad = summed * (1.0 / math.sqrt(steps_count * total_cells))
    new_moment = 0.9 * moment + 0.1 * weight_grad
    new_second = 0.95 * second + 0.05 * weight_grad * weight_grad
    update = new_moment / (jnp.sqrt(new_second) + 1e-08)
    return (grad_input, membrane_grad, weight_grad, new_moment, new_second, update)


def solution(mesh):
    return jax.shard_map(
        on_device,
        mesh=mesh,
        in_specs=(
            P(None, ("dp", "rep"), "space", None, None),
            P(("dp", "rep"), "space", None, None),
            P(None, ("dp", "rep"), "space", None, None),
            P("dp", None),
            P("dp", None),
            P("dp", None),
        ),
        out_specs=(
            P(None, ("dp", "rep"), "space", None, None),
            P(("dp", "rep"), "space", None, None),
            P("dp", None),
            P("dp", None),
            P("dp", None),
            P("dp", None),
        ),
        check_vma=False,
    )
```

```python
import math

import jax
import jax.numpy as jnp
from jax import lax
from jax.sharding import PartitionSpec as P


def extended(x, sides, width):
    for axis, dim in sides:
        peers, length = (lax.axis_size(axis), x.shape[dim])
        up = [(i, (i + 1) % peers) for i in range(peers - 1)]
        down = [(j, i) for i, j in up]
        last = lax.slice_in_dim(x, length - width, length, axis=dim)
        first = lax.slice_in_dim(x, 0, width, axis=dim)
        before = lax.ppermute(last, axis, up)
        after = lax.ppermute(first, axis, down)
        x = jnp.concatenate([before, x, after], axis=dim)
    return x


def doubling_gather(blocks, axis):
    peers = lax.axis_size(axis)
    me = lax.axis_index(axis)
    bit = 0
    while (1 << bit) < peers:
        pairs = [(j, j ^ (1 << bit)) for j in range(peers)]
        other = lax.ppermute(blocks, axis, pairs)
        low = (me // (1 << bit)) % 2 == 0
        blocks = jnp.where(low, jnp.concatenate([blocks, other]), jnp.concatenate([other, blocks]))
        bit += 1
    return blocks


def halving_scatter(blocks, names, stages):
    names = list(names)
    for axis, bit in stages:
        dim = names.index((axis, bit))
        peers = lax.axis_size(axis)
        first = (lax.axis_index(axis) // (1 << bit)) % 2 == 0
        low = lax.index_in_dim(blocks, 0, dim, keepdims=False)
        high = lax.index_in_dim(blocks, 1, dim, keepdims=False)
        pairs = [(j, j ^ (1 << bit)) for j in range(peers)]
        sent = lax.ppermute(jnp.where(first, high, low), axis, pairs)
        blocks = jnp.where(first, low, high) + sent
        names.pop(dim)
    return blocks, names


def bits_of(axis):
    return [(axis, bit) for bit in range(lax.axis_size(axis).bit_length() - 1)]


def surrogate(potential):
    return 1.0 / (1.0 + (math.pi * (potential - 1.0)) ** 2)


def offsets_list():
    return [(row_shift, col_shift) for row_shift in (-1, 0, 1) for col_shift in (-1, 0, 1)]


def on_device(frames, membrane, cotangent, master, moment, second):
    steps_count, samples, rows, cols, chans = frames.shape
    rest = ("space", "rep")
    rest_count = lax.axis_size("space") * lax.axis_size("rep")
    data_count = lax.axis_size("dp")
    shard_rows = master.shape[0]
    piece_rows = shard_rows // rest_count
    local = master.astype(jnp.bfloat16)
    piece = lax.dynamic_slice_in_dim(local, lax.axis_index(rest) * piece_rows, piece_rows, 0)
    over_dp = doubling_gather(piece[None], "dp")
    over_all = lax.all_gather(over_dp, rest, axis=0, tiled=False)
    weights = jnp.swapaxes(over_all, 0, 1).reshape(data_count * shard_rows, master.shape[1])
    stacked = jnp.concatenate([membrane[None], frames], axis=0)
    rimmed = extended(stacked, (("space", 2),), 1)
    voltage = rimmed[0].astype(jnp.float32)
    potentials = []
    fired = []
    for position in range(steps_count):
        potential = 0.5 * voltage + rimmed[position + 1].astype(jnp.float32)
        spikes = jnp.where(potential >= 1.0, jnp.float32(1.0), jnp.float32(0.0))
        voltage = potential - spikes
        potentials.append(potential[:, 1:-1])
        fired.append(spikes)
    potential_all = jnp.stack(potentials)
    spike_all = jnp.stack(fired).astype(jnp.bfloat16)
    col_pad = ((0, 0), (0, 0), (0, 0), (1, 1), (0, 0))
    spike_pad = jnp.pad(spike_all, col_pad)
    grad_rim = extended(cotangent, (("space", 2),), 1)
    grad_pad = jnp.pad(grad_rim, col_pad)
    spike_cols = jnp.concatenate(
        [spike_pad[:, :, 1 + a : 1 + a + rows, 1 + b : 1 + b + cols] for a, b in offsets_list()],
        axis=-1,
    ).reshape(-1, 9 * chans)
    grad_cols = jnp.concatenate(
        [grad_pad[:, :, 1 - a : 1 - a + rows, 1 - b : 1 - b + cols] for a, b in offsets_list()],
        axis=-1,
    ).reshape(-1, 9, chans)
    grad_flat = cotangent.reshape(-1, chans)
    weight_local = lax.dot_general(
        spike_cols, grad_flat, (((0,), (0,)), ((), ())), preferred_element_type=jnp.float32
    )
    dspikes = jnp.einsum(
        "nkd,kcd->nc",
        grad_cols,
        weights.reshape(9, chans, chans),
        preferred_element_type=jnp.float32,
    )
    dspikes = dspikes.reshape(steps_count, samples, rows, cols, chans)
    carried = jnp.zeros((samples, rows, cols, chans), jnp.float32)
    outs = [None] * steps_count
    for position in reversed(range(steps_count)):
        carried = dspikes[position] * surrogate(potential_all[position]) + 0.5 * carried
        outs[position] = (cotangent[position].astype(jnp.float32) + carried).astype(jnp.bfloat16)
    grad_input = jnp.stack(outs)
    membrane_grad = 0.5 * carried
    total_cells = samples * data_count * lax.axis_size("rep") * rows * lax.axis_size("space") * cols
    names = [entry for axis in ("dp",) + rest for entry in reversed(bits_of(axis))]
    piece_shape = (weight_local.shape[0] // 2 ** len(names), weight_local.shape[1])
    blocks = weight_local.reshape((2,) * len(names) + piece_shape)
    space_bits, rep_bits, dp_bits = bits_of("space"), bits_of("rep"), bits_of("dp")
    blocks, names = halving_scatter(blocks, names, space_bits[:1])
    half = chans // 2
    orders = (space_bits[1:] + rep_bits + dp_bits, rep_bits + space_bits[1:] + dp_bits)
    shard_part = jnp.concatenate(
        [
            halving_scatter(blocks[..., part * half : (part + 1) * half], names, order)[0]
            for part, order in enumerate(orders)
        ],
        axis=1,
    )
    summed = lax.all_gather(shard_part, rest, axis=0, tiled=True)
    weight_grad = summed * (1.0 / math.sqrt(steps_count * total_cells))
    new_moment = 0.9 * moment + 0.1 * weight_grad
    new_second = 0.95 * second + 0.05 * weight_grad * weight_grad
    update = new_moment / (jnp.sqrt(new_second) + 1e-08)
    return (grad_input, membrane_grad, weight_grad, new_moment, new_second, update)


def solution(mesh):
    return jax.shard_map(
        on_device,
        mesh=mesh,
        in_specs=(
            P(None, ("dp", "rep"), "space", None, None),
            P(("dp", "rep"), "space", None, None),
            P(None, ("dp", "rep"), "space", None, None),
            P("dp", None),
            P("dp", None),
            P("dp", None),
        ),
        out_specs=(
            P(None, ("dp", "rep"), "space", None, None),
            P(("dp", "rep"), "space", None, None),
            P("dp", None),
            P("dp", None),
            P("dp", None),
            P("dp", None),
        ),
        check_vma=False,
    )
```

```python
import math

import jax
import jax.numpy as jnp
from jax import lax
from jax.sharding import Mesh, PartitionSpec as P
import numpy as np


def extended(x, sides, width):
    for axis, dim in sides:
        peers, length = (size_of(axis), x.shape[dim])
        up = [(i, (i + 1) % peers) for i in range(peers - 1)]
        down = [(j, i) for i, j in up]
        last = lax.slice_in_dim(x, length - width, length, axis=dim)
        first = lax.slice_in_dim(x, 0, width, axis=dim)
        before = lax.ppermute(last, axis, up)
        after = lax.ppermute(first, axis, down)
        x = jnp.concatenate([before, x, after], axis=dim)
    return x


def size_of(axes):
    return math.prod(lax.axis_size(name) for name in axes)


def doubling_gather(blocks, axis):
    peers = size_of(axis)
    me = lax.axis_index(axis)
    bit = 0
    while (1 << bit) < peers:
        pairs = [(j, j ^ (1 << bit)) for j in range(peers)]
        other = lax.ppermute(blocks, axis, pairs)
        low = (me // (1 << bit)) % 2 == 0
        blocks = jnp.where(low, jnp.concatenate([blocks, other]), jnp.concatenate([other, blocks]))
        bit += 1
    return blocks


def surrogate(potential):
    return 1.0 / (1.0 + (math.pi * (potential - 1.0)) ** 2)


def offsets_list():
    return [(row_shift, col_shift) for row_shift in (-1, 0, 1) for col_shift in (-1, 0, 1)]


def build(groups, core):
  dp_axes, space_axes, rep_axes = groups["dp"], groups["space"], groups["rep"]

  def on_device(frames, membrane, cotangent, master, moment, second):
      steps_count, samples, rows, cols, chans = frames.shape
      rest = space_axes + rep_axes
      rest_count = size_of(rest)
      data_count = size_of(dp_axes)
      shard_rows = master.shape[0]
      piece_rows = shard_rows // rest_count
      local = master.astype(jnp.bfloat16)
      piece = lax.dynamic_slice_in_dim(local, lax.axis_index(rest) * piece_rows, piece_rows, 0)
      over_dp = doubling_gather(piece[None], dp_axes)
      over_all = lax.all_gather(over_dp, rest, axis=0, tiled=False)
      weights = jnp.swapaxes(over_all, 0, 1).reshape(data_count * shard_rows, master.shape[1])
      stacked = jnp.concatenate([membrane[None], frames], axis=0)
      rimmed = extended(stacked, ((space_axes, 2),), 1)
      voltage = rimmed[0].astype(jnp.float32)
      potentials = []
      fired = []
      for position in range(steps_count):
          potential = 0.5 * voltage + rimmed[position + 1].astype(jnp.float32)
          spikes = jnp.where(potential >= 1.0, jnp.float32(1.0), jnp.float32(0.0))
          voltage = potential - spikes
          potentials.append(potential[:, 1:-1])
          fired.append(spikes)
      potential_all = jnp.stack(potentials)
      spike_all = jnp.stack(fired).astype(jnp.bfloat16)
      col_pad = ((0, 0), (0, 0), (0, 0), (1, 1), (0, 0))
      spike_pad = jnp.pad(spike_all, col_pad)
      grad_rim = extended(cotangent, ((space_axes, 2),), 1)
      grad_pad = jnp.pad(grad_rim, col_pad)
      spike_cols = jnp.concatenate(
          [spike_pad[:, :, 1 + a : 1 + a + rows, 1 + b : 1 + b + cols] for a, b in offsets_list()],
          axis=-1,
      ).reshape(-1, 9 * chans)
      grad_cols = jnp.concatenate(
          [grad_pad[:, :, 1 - a : 1 - a + rows, 1 - b : 1 - b + cols] for a, b in offsets_list()],
          axis=-1,
      ).reshape(-1, 9, chans)
      grad_flat = cotangent.reshape(-1, chans)
      weight_local = lax.dot_general(
          spike_cols, grad_flat, (((0,), (0,)), ((), ())), preferred_element_type=jnp.float32
      )
      dspikes = jnp.einsum(
          "nkd,kcd->nc",
          grad_cols,
          weights.reshape(9, chans, chans),
          preferred_element_type=jnp.float32,
      )
      dspikes = dspikes.reshape(steps_count, samples, rows, cols, chans)
      carried = jnp.zeros((samples, rows, cols, chans), jnp.float32)
      outs = [None] * steps_count
      for position in reversed(range(steps_count)):
          carried = dspikes[position] * surrogate(potential_all[position]) + 0.5 * carried
          outs[position] = (cotangent[position].astype(jnp.float32) + carried).astype(jnp.bfloat16)
      grad_input = jnp.stack(outs)
      membrane_grad = 0.5 * carried
      total_cells = samples * data_count * size_of(rep_axes) * rows * size_of(space_axes) * cols
      row_axes = dp_axes + rest
      if core is None:
          shard_part = lax.psum_scatter(weight_local, row_axes, scatter_dimension=0, tiled=True)
      else:
          place = row_axes.index(core)
          outer = size_of(row_axes[:place])
          blocks = weight_local.reshape(outer, 2, -1, chans)
          first = lax.axis_index(core) == 0
          low, high = blocks[:, 0], blocks[:, 1]
          sent = lax.ppermute(jnp.where(first, high, low), core, [(0, 1), (1, 0)])
          partial = (jnp.where(first, low, high) + sent).reshape(-1, chans)
          others = row_axes[:place] + row_axes[place + 1 :]
          shard_part = lax.psum_scatter(partial, others, scatter_dimension=0, tiled=True)
      summed = lax.all_gather(shard_part, rest, axis=0, tiled=True)
      weight_grad = summed * (1.0 / math.sqrt(steps_count * total_cells))
      new_moment = 0.9 * moment + 0.1 * weight_grad
      new_second = 0.95 * second + 0.05 * weight_grad * weight_grad
      update = new_moment / (jnp.sqrt(new_second) + 1e-08)
      return (grad_input, membrane_grad, weight_grad, new_moment, new_second, update)

  return on_device


def core_axis(mesh):
    for place, name in enumerate(mesh.axis_names):
        grid = np.moveaxis(mesh.devices, place, -1)
        if grid.shape[-1] % 2:
            continue
        pairs = grid.reshape(-1, 2)
        same = all(
            getattr(a, "coords", None) is not None
            and list(a.coords) == list(b.coords)
            and getattr(a, "core_on_chip", 0) != getattr(b, "core_on_chip", 0)
            for a, b in pairs
        )
        if same:
            return name
    return None


def solution(mesh):
    split = core_axis(mesh)
    groups = {name: (name,) for name in mesh.axis_names}
    core = None
    if split is not None:
        place = list(mesh.axis_names).index(split)
        shape = mesh.devices.shape
        names = list(mesh.axis_names)
        new_names = names[:place] + [split + "_outer", split + "_core"] + names[place + 1 :]
        new_shape = shape[:place] + (shape[place] // 2, 2) + shape[place + 1 :]
        mesh = Mesh(mesh.devices.reshape(new_shape), tuple(new_names))
        groups[split] = (split + "_outer", split + "_core")
        core = split + "_core"

    def spec(*dims):
        out = []
        for dim in dims:
            if dim is None:
                out.append(None)
            else:
                names = dim if isinstance(dim, tuple) else (dim,)
                out.append(tuple(part for name in names for part in groups[name]))
        return P(*out)

    return jax.shard_map(
        build(groups, core),
        mesh=mesh,
        in_specs=(
            spec(None, ("dp", "rep"), "space", None, None),
            spec(("dp", "rep"), "space", None, None),
            spec(None, ("dp", "rep"), "space", None, None),
            spec("dp", None),
            spec("dp", None),
            spec("dp", None),
        ),
        out_specs=(
            spec(None, ("dp", "rep"), "space", None, None),
            spec(("dp", "rep"), "space", None, None),
            spec("dp", None),
            spec("dp", None),
            spec("dp", None),
            spec("dp", None),
        ),
        check_vma=False,
    )
```

```python
import math

import jax
import jax.numpy as jnp
from jax import lax
from jax.sharding import Mesh, PartitionSpec as P
import numpy as np


def extended(x, sides, width):
    for axis, dim in sides:
        peers, length = (size_of(axis), x.shape[dim])
        up = [(i, (i + 1) % peers) for i in range(peers - 1)]
        down = [(j, i) for i, j in up]
        last = lax.slice_in_dim(x, length - width, length, axis=dim)
        first = lax.slice_in_dim(x, 0, width, axis=dim)
        before = lax.ppermute(last, axis, up)
        after = lax.ppermute(first, axis, down)
        x = jnp.concatenate([before, x, after], axis=dim)
    return x


def size_of(axes):
    return math.prod(lax.axis_size(name) for name in axes)


def doubling_gather(blocks, axis):
    peers = size_of(axis)
    me = lax.axis_index(axis)
    bit = 0
    while (1 << bit) < peers:
        pairs = [(j, j ^ (1 << bit)) for j in range(peers)]
        other = lax.ppermute(blocks, axis, pairs)
        low = (me // (1 << bit)) % 2 == 0
        blocks = jnp.where(low, jnp.concatenate([blocks, other]), jnp.concatenate([other, blocks]))
        bit += 1
    return blocks


def surrogate(potential):
    return 1.0 / (1.0 + (math.pi * (potential - 1.0)) ** 2)


def offsets_list():
    return [(row_shift, col_shift) for row_shift in (-1, 0, 1) for col_shift in (-1, 0, 1)]


def build(groups, core):
  dp_axes, space_axes, rep_axes = groups["dp"], groups["space"], groups["rep"]

  def on_device(frames, membrane, cotangent, master, moment, second):
      steps_count, samples, rows, cols, chans = frames.shape
      rest = space_axes + rep_axes
      rest_count = size_of(rest)
      data_count = size_of(dp_axes)
      shard_rows = master.shape[0]
      piece_rows = shard_rows // rest_count
      local = master.astype(jnp.bfloat16)
      piece = lax.dynamic_slice_in_dim(local, lax.axis_index(rest) * piece_rows, piece_rows, 0)
      over_dp = doubling_gather(piece[None], dp_axes)
      over_all = lax.all_gather(over_dp, rest, axis=0, tiled=False)
      weights = jnp.swapaxes(over_all, 0, 1).reshape(data_count * shard_rows, master.shape[1])
      stacked = jnp.concatenate([membrane[None], frames], axis=0)
      rimmed = extended(stacked, ((space_axes, 2),), 1)
      voltage = rimmed[0].astype(jnp.float32)
      potentials = []
      fired = []
      for position in range(steps_count):
          potential = 0.5 * voltage + rimmed[position + 1].astype(jnp.float32)
          spikes = jnp.where(potential >= 1.0, jnp.float32(1.0), jnp.float32(0.0))
          voltage = potential - spikes
          potentials.append(potential[:, 1:-1])
          fired.append(spikes)
      potential_all = jnp.stack(potentials)
      spike_all = jnp.stack(fired).astype(jnp.bfloat16)
      col_pad = ((0, 0), (0, 0), (0, 0), (1, 1), (0, 0))
      spike_pad = jnp.pad(spike_all, col_pad)
      grad_rim = extended(cotangent, ((space_axes, 2),), 1)
      grad_pad = jnp.pad(grad_rim, col_pad)
      spike_cols = jnp.concatenate(
          [spike_pad[:, :, 1 + a : 1 + a + rows, 1 + b : 1 + b + cols] for a, b in offsets_list()],
          axis=-1,
      ).reshape(-1, 9 * chans)
      grad_cols = jnp.concatenate(
          [grad_pad[:, :, 1 - a : 1 - a + rows, 1 - b : 1 - b + cols] for a, b in offsets_list()],
          axis=-1,
      ).reshape(-1, 9, chans)
      grad_flat = cotangent.reshape(-1, chans)
      weight_local = lax.dot_general(
          spike_cols, grad_flat, (((0,), (0,)), ((), ())), preferred_element_type=jnp.float32
      )
      dspikes = jnp.einsum(
          "nkd,kcd->nc",
          grad_cols,
          weights.reshape(9, chans, chans),
          preferred_element_type=jnp.float32,
      )
      dspikes = dspikes.reshape(steps_count, samples, rows, cols, chans)
      carried = jnp.zeros((samples, rows, cols, chans), jnp.float32)
      outs = [None] * steps_count
      for position in reversed(range(steps_count)):
          carried = dspikes[position] * surrogate(potential_all[position]) + 0.5 * carried
          outs[position] = (cotangent[position].astype(jnp.float32) + carried).astype(jnp.bfloat16)
      grad_input = jnp.stack(outs)
      membrane_grad = 0.5 * carried
      total_cells = samples * data_count * size_of(rep_axes) * rows * size_of(space_axes) * cols
      row_axes = dp_axes + rest
      if core is None:
          shard_part = lax.psum_scatter(weight_local, row_axes, scatter_dimension=0, tiled=True)
      else:
          place = row_axes.index(core)
          outer = size_of(row_axes[:place])
          blocks = lax.optimization_barrier(weight_local).reshape(outer, 2, -1, chans)
          first = lax.axis_index(core) == 0
          low, high = blocks[:, 0], blocks[:, 1]
          sent = lax.ppermute(jnp.where(first, high, low), core, [(0, 1), (1, 0)])
          partial = (jnp.where(first, low, high) + sent).reshape(-1, chans)
          others = row_axes[:place] + row_axes[place + 1 :]
          shard_part = lax.psum_scatter(partial, others, scatter_dimension=0, tiled=True)
      summed = lax.all_gather(shard_part, rest, axis=0, tiled=True)
      weight_grad = summed * (1.0 / math.sqrt(steps_count * total_cells))
      new_moment = 0.9 * moment + 0.1 * weight_grad
      new_second = 0.95 * second + 0.05 * weight_grad * weight_grad
      update = new_moment / (jnp.sqrt(new_second) + 1e-08)
      return (grad_input, membrane_grad, weight_grad, new_moment, new_second, update)

  return on_device


def core_axis(mesh):
    for place, name in enumerate(mesh.axis_names):
        grid = np.moveaxis(mesh.devices, place, -1)
        if grid.shape[-1] % 2:
            continue
        pairs = grid.reshape(-1, 2)
        same = all(
            getattr(a, "coords", None) is not None
            and list(a.coords) == list(b.coords)
            and getattr(a, "core_on_chip", 0) != getattr(b, "core_on_chip", 0)
            for a, b in pairs
        )
        if same:
            return name
    return None


def solution(mesh):
    split = core_axis(mesh)
    groups = {name: (name,) for name in mesh.axis_names}
    core = None
    if split is not None:
        place = list(mesh.axis_names).index(split)
        shape = mesh.devices.shape
        names = list(mesh.axis_names)
        new_names = names[:place] + [split + "_outer", split + "_core"] + names[place + 1 :]
        new_shape = shape[:place] + (shape[place] // 2, 2) + shape[place + 1 :]
        mesh = Mesh(mesh.devices.reshape(new_shape), tuple(new_names))
        groups[split] = (split + "_outer", split + "_core")
        core = split + "_core"

    def spec(*dims):
        out = []
        for dim in dims:
            if dim is None:
                out.append(None)
            else:
                names = dim if isinstance(dim, tuple) else (dim,)
                out.append(tuple(part for name in names for part in groups[name]))
        return P(*out)

    return jax.shard_map(
        build(groups, core),
        mesh=mesh,
        in_specs=(
            spec(None, ("dp", "rep"), "space", None, None),
            spec(("dp", "rep"), "space", None, None),
            spec(None, ("dp", "rep"), "space", None, None),
            spec("dp", None),
            spec("dp", None),
            spec("dp", None),
        ),
        out_specs=(
            spec(None, ("dp", "rep"), "space", None, None),
            spec(("dp", "rep"), "space", None, None),
            spec("dp", None),
            spec("dp", None),
            spec("dp", None),
            spec("dp", None),
        ),
        check_vma=False,
    )
```

```python
import math

import jax
import jax.numpy as jnp
from jax import lax
from jax.sharding import PartitionSpec as P


def extended(x, sides, width):
    for axis, dim in sides:
        peers, length = (lax.axis_size(axis), x.shape[dim])
        up = [(i, (i + 1) % peers) for i in range(peers - 1)]
        down = [(j, i) for i, j in up]
        last = lax.slice_in_dim(x, length - width, length, axis=dim)
        first = lax.slice_in_dim(x, 0, width, axis=dim)
        before = lax.ppermute(last, axis, up)
        after = lax.ppermute(first, axis, down)
        x = jnp.concatenate([before, x, after], axis=dim)
    return x


def doubling_gather(blocks, axis):
    peers = lax.axis_size(axis)
    me = lax.axis_index(axis)
    bit = 0
    while (1 << bit) < peers:
        pairs = [(j, j ^ (1 << bit)) for j in range(peers)]
        other = lax.ppermute(blocks, axis, pairs)
        low = (me // (1 << bit)) % 2 == 0
        blocks = jnp.where(low, jnp.concatenate([blocks, other]), jnp.concatenate([other, blocks]))
        bit += 1
    return blocks


def halving_scatter(blocks, names, stages):
    names = list(names)
    for axis, bit in stages:
        dim = names.index((axis, bit))
        peers = lax.axis_size(axis)
        first = (lax.axis_index(axis) // (1 << bit)) % 2 == 0
        low = lax.index_in_dim(blocks, 0, dim, keepdims=False)
        high = lax.index_in_dim(blocks, 1, dim, keepdims=False)
        pairs = [(j, j ^ (1 << bit)) for j in range(peers)]
        sent = lax.ppermute(jnp.where(first, high, low), axis, pairs)
        blocks = jnp.where(first, low, high) + sent
        names.pop(dim)
    return blocks, names


def bits_of(axis):
    return [(axis, bit) for bit in range(lax.axis_size(axis).bit_length() - 1)]


def surrogate(potential):
    return 1.0 / (1.0 + (math.pi * (potential - 1.0)) ** 2)


def offsets_list():
    return [(row_shift, col_shift) for row_shift in (-1, 0, 1) for col_shift in (-1, 0, 1)]


def on_device(frames, membrane, cotangent, master, moment, second):
    steps_count, samples, rows, cols, chans = frames.shape
    rest = ("space", "rep")
    rest_count = lax.axis_size("space") * lax.axis_size("rep")
    data_count = lax.axis_size("dp")
    shard_rows = master.shape[0]
    piece_rows = shard_rows // rest_count
    local = master.astype(jnp.bfloat16)
    piece = lax.dynamic_slice_in_dim(local, lax.axis_index(rest) * piece_rows, piece_rows, 0)
    over_dp = doubling_gather(piece[None], "dp")
    over_all = lax.all_gather(over_dp, rest, axis=0, tiled=False)
    weights = jnp.swapaxes(over_all, 0, 1).reshape(data_count * shard_rows, master.shape[1])
    stacked = jnp.concatenate([membrane[None], frames], axis=0)
    rimmed = extended(stacked, (("space", 2),), 1)
    voltage = rimmed[0].astype(jnp.float32)
    potentials = []
    fired = []
    for position in range(steps_count):
        potential = 0.5 * voltage + rimmed[position + 1].astype(jnp.float32)
        spikes = jnp.where(potential >= 1.0, jnp.float32(1.0), jnp.float32(0.0))
        voltage = potential - spikes
        potentials.append(potential[:, 1:-1])
        fired.append(spikes)
    potential_all = jnp.stack(potentials)
    spike_all = jnp.stack(fired).astype(jnp.bfloat16)
    col_pad = ((0, 0), (0, 0), (0, 0), (1, 1), (0, 0))
    spike_pad = jnp.pad(spike_all, col_pad)
    grad_rim = extended(cotangent, (("space", 2),), 1)
    grad_pad = jnp.pad(grad_rim, col_pad)
    spike_cols = jnp.concatenate(
        [spike_pad[:, :, 1 + a : 1 + a + rows, 1 + b : 1 + b + cols] for a, b in offsets_list()],
        axis=-1,
    ).reshape(-1, 9 * chans)
    grad_cols = jnp.concatenate(
        [grad_pad[:, :, 1 - a : 1 - a + rows, 1 - b : 1 - b + cols] for a, b in offsets_list()],
        axis=-1,
    ).reshape(-1, 9, chans)
    grad_flat = cotangent.reshape(-1, chans)
    weight_local = lax.dot_general(
        spike_cols, grad_flat, (((0,), (0,)), ((), ())), preferred_element_type=jnp.float32
    )
    dspikes = jnp.einsum(
        "nkd,kcd->nc",
        grad_cols,
        weights.reshape(9, chans, chans),
        preferred_element_type=jnp.float32,
    )
    dspikes = dspikes.reshape(steps_count, samples, rows, cols, chans)
    carried = jnp.zeros((samples, rows, cols, chans), jnp.float32)
    outs = [None] * steps_count
    for position in reversed(range(steps_count)):
        carried = dspikes[position] * surrogate(potential_all[position]) + 0.5 * carried
        outs[position] = (cotangent[position].astype(jnp.float32) + carried).astype(jnp.bfloat16)
    grad_input = jnp.stack(outs)
    membrane_grad = 0.5 * carried
    total_cells = samples * data_count * lax.axis_size("rep") * rows * lax.axis_size("space") * cols
    names = [entry for axis in ("dp",) + rest for entry in reversed(bits_of(axis))]
    piece_shape = (weight_local.shape[0] // 2 ** len(names), weight_local.shape[1])
    blocks = lax.optimization_barrier(weight_local).reshape((2,) * len(names) + piece_shape)
    space_bits, rep_bits, dp_bits = bits_of("space"), bits_of("rep"), bits_of("dp")
    blocks, names = halving_scatter(blocks, names, space_bits[:1])
    half = chans // 2
    orders = (space_bits[1:] + rep_bits + dp_bits, rep_bits + space_bits[1:] + dp_bits)
    shard_part = jnp.concatenate(
        [
            halving_scatter(blocks[..., part * half : (part + 1) * half], names, order)[0]
            for part, order in enumerate(orders)
        ],
        axis=1,
    )
    summed = lax.all_gather(shard_part, rest, axis=0, tiled=True)
    weight_grad = summed * (1.0 / math.sqrt(steps_count * total_cells))
    new_moment = 0.9 * moment + 0.1 * weight_grad
    new_second = 0.95 * second + 0.05 * weight_grad * weight_grad
    update = new_moment / (jnp.sqrt(new_second) + 1e-08)
    return (grad_input, membrane_grad, weight_grad, new_moment, new_second, update)


def solution(mesh):
    return jax.shard_map(
        on_device,
        mesh=mesh,
        in_specs=(
            P(None, ("dp", "rep"), "space", None, None),
            P(("dp", "rep"), "space", None, None),
            P(None, ("dp", "rep"), "space", None, None),
            P("dp", None),
            P("dp", None),
            P("dp", None),
        ),
        out_specs=(
            P(None, ("dp", "rep"), "space", None, None),
            P(("dp", "rep"), "space", None, None),
            P("dp", None),
            P("dp", None),
            P("dp", None),
            P("dp", None),
        ),
        check_vma=False,
    )
```

```python
import math

import jax
import jax.numpy as jnp
from jax import lax
from jax.sharding import PartitionSpec as P


def extended(x, sides, width):
    for axis, dim in sides:
        peers, length = (lax.axis_size(axis), x.shape[dim])
        up = [(i, (i + 1) % peers) for i in range(peers - 1)]
        down = [(j, i) for i, j in up]
        last = lax.slice_in_dim(x, length - width, length, axis=dim)
        first = lax.slice_in_dim(x, 0, width, axis=dim)
        before = lax.ppermute(last, axis, up)
        after = lax.ppermute(first, axis, down)
        x = jnp.concatenate([before, x, after], axis=dim)
    return x


def doubling_gather(blocks, axis):
    peers = lax.axis_size(axis)
    me = lax.axis_index(axis)
    bit = 0
    while (1 << bit) < peers:
        pairs = [(j, j ^ (1 << bit)) for j in range(peers)]
        other = lax.ppermute(blocks, axis, pairs)
        low = (me // (1 << bit)) % 2 == 0
        blocks = jnp.where(low, jnp.concatenate([blocks, other]), jnp.concatenate([other, blocks]))
        bit += 1
    return blocks


def halving_scatter(blocks, names, stages):
    names = list(names)
    for axis, bit in stages:
        dim = names.index((axis, bit))
        peers = lax.axis_size(axis)
        first = (lax.axis_index(axis) // (1 << bit)) % 2 == 0
        low = lax.index_in_dim(blocks, 0, dim, keepdims=False)
        high = lax.index_in_dim(blocks, 1, dim, keepdims=False)
        pairs = [(j, j ^ (1 << bit)) for j in range(peers)]
        sent = lax.ppermute(jnp.where(first, high, low), axis, pairs)
        blocks = jnp.where(first, low, high) + sent
        names.pop(dim)
    return blocks, names


def bits_of(axis):
    return [(axis, bit) for bit in range(lax.axis_size(axis).bit_length() - 1)]


def surrogate(potential):
    return 1.0 / (1.0 + (math.pi * (potential - 1.0)) ** 2)


def offsets_list():
    return [(row_shift, col_shift) for row_shift in (-1, 0, 1) for col_shift in (-1, 0, 1)]


def on_device(frames, membrane, cotangent, master, moment, second):
    steps_count, samples, rows, cols, chans = frames.shape
    rest = ("space", "rep")
    rest_count = lax.axis_size("space") * lax.axis_size("rep")
    data_count = lax.axis_size("dp")
    shard_rows = master.shape[0]
    piece_rows = shard_rows // rest_count
    weights = doubling_gather(master.astype(jnp.bfloat16)[None], "dp").reshape(-1, master.shape[1])
    stacked = jnp.concatenate([membrane[None], frames], axis=0)
    rimmed = extended(stacked, (("space", 2),), 1)
    voltage = rimmed[0].astype(jnp.float32)
    potentials = []
    fired = []
    for position in range(steps_count):
        potential = 0.5 * voltage + rimmed[position + 1].astype(jnp.float32)
        spikes = jnp.where(potential >= 1.0, jnp.float32(1.0), jnp.float32(0.0))
        voltage = potential - spikes
        potentials.append(potential[:, 1:-1])
        fired.append(spikes)
    potential_all = jnp.stack(potentials)
    spike_all = jnp.stack(fired).astype(jnp.bfloat16)
    col_pad = ((0, 0), (0, 0), (0, 0), (1, 1), (0, 0))
    spike_pad = jnp.pad(spike_all, col_pad)
    grad_rim = extended(cotangent, (("space", 2),), 1)
    grad_pad = jnp.pad(grad_rim, col_pad)
    spike_cols = jnp.concatenate(
        [spike_pad[:, :, 1 + a : 1 + a + rows, 1 + b : 1 + b + cols] for a, b in offsets_list()],
        axis=-1,
    ).reshape(-1, 9 * chans)
    grad_cols = jnp.concatenate(
        [grad_pad[:, :, 1 - a : 1 - a + rows, 1 - b : 1 - b + cols] for a, b in offsets_list()],
        axis=-1,
    ).reshape(-1, 9, chans)
    grad_flat = cotangent.reshape(-1, chans)
    weight_local = lax.dot_general(
        spike_cols, grad_flat, (((0,), (0,)), ((), ())), preferred_element_type=jnp.float32
    )
    dspikes = jnp.einsum(
        "nkd,kcd->nc",
        grad_cols,
        weights.reshape(9, chans, chans),
        preferred_element_type=jnp.float32,
    )
    dspikes = dspikes.reshape(steps_count, samples, rows, cols, chans)
    carried = jnp.zeros((samples, rows, cols, chans), jnp.float32)
    outs = [None] * steps_count
    for position in reversed(range(steps_count)):
        carried = dspikes[position] * surrogate(potential_all[position]) + 0.5 * carried
        outs[position] = (cotangent[position].astype(jnp.float32) + carried).astype(jnp.bfloat16)
    grad_input = jnp.stack(outs)
    membrane_grad = 0.5 * carried
    total_cells = samples * data_count * lax.axis_size("rep") * rows * lax.axis_size("space") * cols
    names = [entry for axis in ("dp",) + rest for entry in reversed(bits_of(axis))]
    piece_shape = (weight_local.shape[0] // 2 ** len(names), weight_local.shape[1])
    space_bits, rep_bits, dp_bits = bits_of("space"), bits_of("rep"), bits_of("dp")
    place = names.index(space_bits[0])
    view = lax.optimization_barrier(weight_local).reshape(2**place, 2, -1, chans)
    first = lax.axis_index("space") % 2 == 0
    low, high = view[:, 0], view[:, 1]
    sent = lax.ppermute(jnp.where(first, high, low), "space", [(j, j ^ 1) for j in range(lax.axis_size("space"))])
    partial = jnp.where(first, low, high) + sent
    names.pop(place)
    blocks = partial.reshape((2,) * len(names) + piece_shape)
    half = chans // 2
    orders = (space_bits[1:] + rep_bits + dp_bits, rep_bits + space_bits[1:] + dp_bits)
    shard_part = jnp.concatenate(
        [
            halving_scatter(blocks[..., part * half : (part + 1) * half], names, order)[0]
            for part, order in enumerate(orders)
        ],
        axis=1,
    )
    summed = lax.all_gather(shard_part, rest, axis=0, tiled=True)
    weight_grad = summed * (1.0 / math.sqrt(steps_count * total_cells))
    new_moment = 0.9 * moment + 0.1 * weight_grad
    new_second = 0.95 * second + 0.05 * weight_grad * weight_grad
    update = new_moment / (jnp.sqrt(new_second) + 1e-08)
    return (grad_input, membrane_grad, weight_grad, new_moment, new_second, update)


def solution(mesh):
    return jax.shard_map(
        on_device,
        mesh=mesh,
        in_specs=(
            P(None, ("dp", "rep"), "space", None, None),
            P(("dp", "rep"), "space", None, None),
            P(None, ("dp", "rep"), "space", None, None),
            P("dp", None),
            P("dp", None),
            P("dp", None),
        ),
        out_specs=(
            P(None, ("dp", "rep"), "space", None, None),
            P(("dp", "rep"), "space", None, None),
            P("dp", None),
            P("dp", None),
            P("dp", None),
            P("dp", None),
        ),
        check_vma=False,
    )
```

```python
import math

import jax
import jax.numpy as jnp
from jax import lax
from jax.sharding import PartitionSpec as P


def extended(x, sides, width):
    for axis, dim in sides:
        peers, length = (lax.axis_size(axis), x.shape[dim])
        up = [(i, (i + 1) % peers) for i in range(peers - 1)]
        down = [(j, i) for i, j in up]
        last = lax.slice_in_dim(x, length - width, length, axis=dim)
        first = lax.slice_in_dim(x, 0, width, axis=dim)
        before = lax.ppermute(last, axis, up)
        after = lax.ppermute(first, axis, down)
        x = jnp.concatenate([before, x, after], axis=dim)
    return x


def doubling_gather(blocks, axis):
    peers = lax.axis_size(axis)
    me = lax.axis_index(axis)
    bit = 0
    while (1 << bit) < peers:
        pairs = [(j, j ^ (1 << bit)) for j in range(peers)]
        other = lax.ppermute(blocks, axis, pairs)
        low = (me // (1 << bit)) % 2 == 0
        blocks = jnp.where(low, jnp.concatenate([blocks, other]), jnp.concatenate([other, blocks]))
        bit += 1
    return blocks


def halving_scatter(blocks, names, stages):
    names = list(names)
    for axis, bit in stages:
        dim = names.index((axis, bit))
        peers = lax.axis_size(axis)
        first = (lax.axis_index(axis) // (1 << bit)) % 2 == 0
        low = lax.index_in_dim(blocks, 0, dim, keepdims=False)
        high = lax.index_in_dim(blocks, 1, dim, keepdims=False)
        pairs = [(j, j ^ (1 << bit)) for j in range(peers)]
        sent = lax.ppermute(jnp.where(first, high, low), axis, pairs)
        blocks = jnp.where(first, low, high) + sent
        names.pop(dim)
    return blocks, names


def bits_of(axis):
    return [(axis, bit) for bit in range(lax.axis_size(axis).bit_length() - 1)]


def surrogate(potential):
    return 1.0 / (1.0 + (math.pi * (potential - 1.0)) ** 2)


def offsets_list():
    return [(row_shift, col_shift) for row_shift in (-1, 0, 1) for col_shift in (-1, 0, 1)]


def on_device(frames, membrane, cotangent, master, moment, second):
    steps_count, samples, rows, cols, chans = frames.shape
    rest = ("space", "rep")
    rest_count = lax.axis_size("space") * lax.axis_size("rep")
    data_count = lax.axis_size("dp")
    shard_rows = master.shape[0]
    piece_rows = shard_rows // rest_count
    local = master.astype(jnp.bfloat16)
    piece = lax.dynamic_slice_in_dim(local, lax.axis_index(rest) * piece_rows, piece_rows, 0)
    over_dp = doubling_gather(piece[None], "dp")
    over_all = lax.all_gather(over_dp, rest, axis=0, tiled=False)
    weights = jnp.swapaxes(over_all, 0, 1).reshape(data_count * shard_rows, master.shape[1])
    stacked = jnp.concatenate([membrane[None], frames], axis=0)
    rimmed = extended(stacked, (("space", 2),), 1)
    voltage = rimmed[0].astype(jnp.float32)
    potentials = []
    fired = []
    for position in range(steps_count):
        potential = 0.5 * voltage + rimmed[position + 1].astype(jnp.float32)
        spikes = jnp.where(potential >= 1.0, jnp.float32(1.0), jnp.float32(0.0))
        voltage = potential - spikes
        potentials.append(potential[:, 1:-1])
        fired.append(spikes)
    potential_all = jnp.stack(potentials)
    spike_all = jnp.stack(fired).astype(jnp.bfloat16)
    col_pad = ((0, 0), (0, 0), (0, 0), (1, 1), (0, 0))
    spike_pad = jnp.pad(spike_all, col_pad)
    grad_rim = extended(cotangent, (("space", 2),), 1)
    grad_pad = jnp.pad(grad_rim, col_pad)
    spike_cols = jnp.concatenate(
        [spike_pad[:, :, 1 + a : 1 + a + rows, 1 + b : 1 + b + cols] for a, b in offsets_list()],
        axis=-1,
    ).reshape(-1, 9 * chans)
    grad_cols = jnp.concatenate(
        [grad_pad[:, :, 1 - a : 1 - a + rows, 1 - b : 1 - b + cols] for a, b in offsets_list()],
        axis=-1,
    ).reshape(-1, 9, chans)
    grad_flat = cotangent.reshape(-1, chans)
    weight_local = lax.dot_general(
        spike_cols, grad_flat, (((0,), (0,)), ((), ())), preferred_element_type=jnp.float32
    )
    dspikes = jnp.einsum(
        "nkd,kcd->nc",
        grad_cols,
        weights.reshape(9, chans, chans),
        preferred_element_type=jnp.float32,
    )
    dspikes = dspikes.reshape(steps_count, samples, rows, cols, chans)
    carried = jnp.zeros((samples, rows, cols, chans), jnp.float32)
    outs = [None] * steps_count
    for position in reversed(range(steps_count)):
        carried = dspikes[position] * surrogate(potential_all[position]) + 0.5 * carried
        outs[position] = (cotangent[position].astype(jnp.float32) + carried).astype(jnp.bfloat16)
    grad_input = jnp.stack(outs)
    membrane_grad = 0.5 * carried
    total_cells = samples * data_count * lax.axis_size("rep") * rows * lax.axis_size("space") * cols
    names = [entry for axis in ("dp",) + rest for entry in reversed(bits_of(axis))]
    piece_shape = (weight_local.shape[0] // 2 ** len(names), weight_local.shape[1])
    space_bits, rep_bits, dp_bits = bits_of("space"), bits_of("rep"), bits_of("dp")
    place = names.index(space_bits[0])
    view = lax.optimization_barrier(weight_local).reshape(2**place, 2, -1, chans)
    first = lax.axis_index("space") % 2 == 0
    low, high = view[:, 0], view[:, 1]
    sent = lax.ppermute(jnp.where(first, high, low), "space", [(j, j ^ 1) for j in range(lax.axis_size("space"))])
    partial = jnp.where(first, low, high) + sent
    names.pop(place)
    blocks = partial.reshape((2,) * len(names) + piece_shape)
    half = chans // 2
    orders = (space_bits[1:] + rep_bits + dp_bits, rep_bits + space_bits[1:] + dp_bits)
    shard_part = jnp.concatenate(
        [
            halving_scatter(blocks[..., part * half : (part + 1) * half], names, order)[0]
            for part, order in enumerate(orders)
        ],
        axis=1,
    )
    summed = lax.all_gather(shard_part, rest, axis=0, tiled=True)
    weight_grad = summed * (1.0 / math.sqrt(steps_count * total_cells))
    new_moment = 0.9 * moment + 0.1 * weight_grad
    new_second = 0.95 * second + 0.05 * weight_grad * weight_grad
    update = new_moment / (jnp.sqrt(new_second) + 1e-08)
    return (grad_input, membrane_grad, weight_grad, new_moment, new_second, update)


def solution(mesh):
    return jax.shard_map(
        on_device,
        mesh=mesh,
        in_specs=(
            P(None, ("dp", "rep"), "space", None, None),
            P(("dp", "rep"), "space", None, None),
            P(None, ("dp", "rep"), "space", None, None),
            P("dp", None),
            P("dp", None),
            P("dp", None),
        ),
        out_specs=(
            P(None, ("dp", "rep"), "space", None, None),
            P(("dp", "rep"), "space", None, None),
            P("dp", None),
            P("dp", None),
            P("dp", None),
            P("dp", None),
        ),
        check_vma=False,
    )
```

```python
import math

import jax
import jax.numpy as jnp
from jax import lax
from jax.sharding import PartitionSpec as P


def extended(x, sides, width):
    for axis, dim in sides:
        peers, length = (lax.axis_size(axis), x.shape[dim])
        up = [(i, (i + 1) % peers) for i in range(peers - 1)]
        down = [(j, i) for i, j in up]
        last = lax.slice_in_dim(x, length - width, length, axis=dim)
        first = lax.slice_in_dim(x, 0, width, axis=dim)
        before = lax.ppermute(last, axis, up)
        after = lax.ppermute(first, axis, down)
        x = jnp.concatenate([before, x, after], axis=dim)
    return x


def doubling_gather(blocks, axis):
    peers = lax.axis_size(axis)
    me = lax.axis_index(axis)
    bit = 0
    while (1 << bit) < peers:
        pairs = [(j, j ^ (1 << bit)) for j in range(peers)]
        other = lax.ppermute(blocks, axis, pairs)
        low = (me // (1 << bit)) % 2 == 0
        blocks = jnp.where(low, jnp.concatenate([blocks, other]), jnp.concatenate([other, blocks]))
        bit += 1
    return blocks


def halving_scatter(blocks, names, stages):
    names = list(names)
    for axis, bit in stages:
        dim = names.index((axis, bit))
        peers = lax.axis_size(axis)
        first = (lax.axis_index(axis) // (1 << bit)) % 2 == 0
        low = lax.index_in_dim(blocks, 0, dim, keepdims=False)
        high = lax.index_in_dim(blocks, 1, dim, keepdims=False)
        pairs = [(j, j ^ (1 << bit)) for j in range(peers)]
        sent = lax.ppermute(jnp.where(first, high, low), axis, pairs)
        blocks = jnp.where(first, low, high) + sent
        names.pop(dim)
    return blocks, names


def bits_of(axis):
    return [(axis, bit) for bit in range(lax.axis_size(axis).bit_length() - 1)]


def staged_gather(blocks, stages):
    for axis, bit in stages:
        peers = lax.axis_size(axis)
        pairs = [(j, j ^ (1 << bit)) for j in range(peers)]
        other = lax.ppermute(blocks, axis, pairs)
        low = (lax.axis_index(axis) // (1 << bit)) % 2 == 0
        blocks = jnp.where(low, jnp.stack([blocks, other]), jnp.stack([other, blocks]))
    return blocks


def rest_gather(blocks, axes):
    natural = [(axis, bit) for axis in axes for bit in reversed(range(lax.axis_size(axis).bit_length() - 1))]
    stages = natural[::-1]
    stages = [e for e in stages if e[0] != "space"] + [e for e in natural if e[0] == "space"]
    gathered = staged_gather(blocks, stages)
    held = stages[::-1]
    order = [held.index(entry) for entry in natural]
    gathered = jnp.transpose(gathered, order + list(range(len(stages), gathered.ndim)))
    return gathered.reshape((2 ** len(stages),) + blocks.shape)


def surrogate(potential):
    return 1.0 / (1.0 + (math.pi * (potential - 1.0)) ** 2)


def offsets_list():
    return [(row_shift, col_shift) for row_shift in (-1, 0, 1) for col_shift in (-1, 0, 1)]


def on_device(frames, membrane, cotangent, master, moment, second):
    steps_count, samples, rows, cols, chans = frames.shape
    rest = ("space", "rep")
    rest_count = lax.axis_size("space") * lax.axis_size("rep")
    data_count = lax.axis_size("dp")
    shard_rows = master.shape[0]
    piece_rows = shard_rows // rest_count
    local = master.astype(jnp.bfloat16)
    piece = lax.dynamic_slice_in_dim(local, lax.axis_index(rest) * piece_rows, piece_rows, 0)
    over_dp = doubling_gather(piece[None], "dp")
    over_all = rest_gather(over_dp, rest)
    weights = jnp.swapaxes(over_all, 0, 1).reshape(data_count * shard_rows, master.shape[1])
    stacked = jnp.concatenate([membrane[None], frames], axis=0)
    rimmed = extended(stacked, (("space", 2),), 1)
    voltage = rimmed[0].astype(jnp.float32)
    potentials = []
    fired = []
    for position in range(steps_count):
        potential = 0.5 * voltage + rimmed[position + 1].astype(jnp.float32)
        spikes = jnp.where(potential >= 1.0, jnp.float32(1.0), jnp.float32(0.0))
        voltage = potential - spikes
        potentials.append(potential[:, 1:-1])
        fired.append(spikes)
    potential_all = jnp.stack(potentials)
    spike_all = jnp.stack(fired).astype(jnp.bfloat16)
    col_pad = ((0, 0), (0, 0), (0, 0), (1, 1), (0, 0))
    spike_pad = jnp.pad(spike_all, col_pad)
    grad_rim = extended(cotangent, (("space", 2),), 1)
    grad_pad = jnp.pad(grad_rim, col_pad)
    spike_cols = jnp.concatenate(
        [spike_pad[:, :, 1 + a : 1 + a + rows, 1 + b : 1 + b + cols] for a, b in offsets_list()],
        axis=-1,
    ).reshape(-1, 9 * chans)
    grad_cols = jnp.concatenate(
        [grad_pad[:, :, 1 - a : 1 - a + rows, 1 - b : 1 - b + cols] for a, b in offsets_list()],
        axis=-1,
    ).reshape(-1, 9, chans)
    grad_flat = cotangent.reshape(-1, chans)
    weight_local = lax.dot_general(
        spike_cols, grad_flat, (((0,), (0,)), ((), ())), preferred_element_type=jnp.float32
    )
    dspikes = jnp.einsum(
        "nkd,kcd->nc",
        grad_cols,
        weights.reshape(9, chans, chans),
        preferred_element_type=jnp.float32,
    )
    dspikes = dspikes.reshape(steps_count, samples, rows, cols, chans)
    carried = jnp.zeros((samples, rows, cols, chans), jnp.float32)
    outs = [None] * steps_count
    for position in reversed(range(steps_count)):
        carried = dspikes[position] * surrogate(potential_all[position]) + 0.5 * carried
        outs[position] = (cotangent[position].astype(jnp.float32) + carried).astype(jnp.bfloat16)
    grad_input = jnp.stack(outs)
    membrane_grad = 0.5 * carried
    total_cells = samples * data_count * lax.axis_size("rep") * rows * lax.axis_size("space") * cols
    names = [entry for axis in ("dp",) + rest for entry in reversed(bits_of(axis))]
    piece_shape = (weight_local.shape[0] // 2 ** len(names), weight_local.shape[1])
    blocks = lax.optimization_barrier(weight_local).reshape((2,) * len(names) + piece_shape)
    space_bits, rep_bits, dp_bits = bits_of("space"), bits_of("rep"), bits_of("dp")
    blocks, names = halving_scatter(blocks, names, space_bits[:1])
    half = chans // 2
    orders = (space_bits[1:] + rep_bits + dp_bits, rep_bits + space_bits[1:] + dp_bits)
    shard_part = jnp.concatenate(
        [
            halving_scatter(blocks[..., part * half : (part + 1) * half], names, order)[0]
            for part, order in enumerate(orders)
        ],
        axis=1,
    )
    summed = rest_gather(shard_part, rest).reshape(-1, chans)
    weight_grad = summed * (1.0 / math.sqrt(steps_count * total_cells))
    new_moment = 0.9 * moment + 0.1 * weight_grad
    new_second = 0.95 * second + 0.05 * weight_grad * weight_grad
    update = new_moment / (jnp.sqrt(new_second) + 1e-08)
    return (grad_input, membrane_grad, weight_grad, new_moment, new_second, update)


def solution(mesh):
    return jax.shard_map(
        on_device,
        mesh=mesh,
        in_specs=(
            P(None, ("dp", "rep"), "space", None, None),
            P(("dp", "rep"), "space", None, None),
            P(None, ("dp", "rep"), "space", None, None),
            P("dp", None),
            P("dp", None),
            P("dp", None),
        ),
        out_specs=(
            P(None, ("dp", "rep"), "space", None, None),
            P(("dp", "rep"), "space", None, None),
            P("dp", None),
            P("dp", None),
            P("dp", None),
            P("dp", None),
        ),
        check_vma=False,
    )
```

```python
import math

import jax
import jax.numpy as jnp
from jax import lax
from jax.sharding import PartitionSpec as P


def extended(x, sides, width):
    for axis, dim in sides:
        peers, length = (lax.axis_size(axis), x.shape[dim])
        up = [(i, (i + 1) % peers) for i in range(peers - 1)]
        down = [(j, i) for i, j in up]
        last = lax.slice_in_dim(x, length - width, length, axis=dim)
        first = lax.slice_in_dim(x, 0, width, axis=dim)
        before = lax.ppermute(last, axis, up)
        after = lax.ppermute(first, axis, down)
        x = jnp.concatenate([before, x, after], axis=dim)
    return x


def doubling_gather(blocks, axis):
    peers = lax.axis_size(axis)
    me = lax.axis_index(axis)
    bit = 0
    while (1 << bit) < peers:
        pairs = [(j, j ^ (1 << bit)) for j in range(peers)]
        other = lax.ppermute(blocks, axis, pairs)
        low = (me // (1 << bit)) % 2 == 0
        blocks = jnp.where(low, jnp.concatenate([blocks, other]), jnp.concatenate([other, blocks]))
        bit += 1
    return blocks


def halving_scatter(blocks, names, stages):
    names = list(names)
    for axis, bit in stages:
        dim = names.index((axis, bit))
        peers = lax.axis_size(axis)
        first = (lax.axis_index(axis) // (1 << bit)) % 2 == 0
        low = lax.index_in_dim(blocks, 0, dim, keepdims=False)
        high = lax.index_in_dim(blocks, 1, dim, keepdims=False)
        pairs = [(j, j ^ (1 << bit)) for j in range(peers)]
        sent = lax.ppermute(jnp.where(first, high, low), axis, pairs)
        blocks = jnp.where(first, low, high) + sent
        names.pop(dim)
    return blocks, names


def bits_of(axis):
    return [(axis, bit) for bit in range(lax.axis_size(axis).bit_length() - 1)]


def surrogate(potential):
    return 1.0 / (1.0 + (math.pi * (potential - 1.0)) ** 2)


def offsets_list():
    return [(row_shift, col_shift) for row_shift in (-1, 0, 1) for col_shift in (-1, 0, 1)]


def on_device(frames, membrane, cotangent, master, moment, second):
    steps_count, samples, rows, cols, chans = frames.shape
    rest = ("space", "rep")
    rest_count = lax.axis_size("space") * lax.axis_size("rep")
    data_count = lax.axis_size("dp")
    shard_rows = master.shape[0]
    piece_rows = shard_rows // rest_count
    local = master.astype(jnp.bfloat16)
    piece = lax.dynamic_slice_in_dim(local, lax.axis_index(rest) * piece_rows, piece_rows, 0)
    weights = lax.all_gather(piece, ("dp",) + rest, axis=0, tiled=True)
    stacked = jnp.concatenate([membrane[None], frames], axis=0)
    rimmed = extended(stacked, (("space", 2),), 1)
    voltage = rimmed[0].astype(jnp.float32)
    potentials = []
    fired = []
    for position in range(steps_count):
        potential = 0.5 * voltage + rimmed[position + 1].astype(jnp.float32)
        spikes = jnp.where(potential >= 1.0, jnp.float32(1.0), jnp.float32(0.0))
        voltage = potential - spikes
        potentials.append(potential[:, 1:-1])
        fired.append(spikes)
    potential_all = jnp.stack(potentials)
    spike_all = jnp.stack(fired).astype(jnp.bfloat16)
    col_pad = ((0, 0), (0, 0), (0, 0), (1, 1), (0, 0))
    spike_pad = jnp.pad(spike_all, col_pad)
    grad_rim = extended(cotangent, (("space", 2),), 1)
    grad_pad = jnp.pad(grad_rim, col_pad)
    spike_cols = jnp.concatenate(
        [spike_pad[:, :, 1 + a : 1 + a + rows, 1 + b : 1 + b + cols] for a, b in offsets_list()],
        axis=-1,
    ).reshape(-1, 9 * chans)
    grad_cols = jnp.concatenate(
        [grad_pad[:, :, 1 - a : 1 - a + rows, 1 - b : 1 - b + cols] for a, b in offsets_list()],
        axis=-1,
    ).reshape(-1, 9, chans)
    grad_flat = cotangent.reshape(-1, chans)
    weight_local = lax.dot_general(
        spike_cols, grad_flat, (((0,), (0,)), ((), ())), preferred_element_type=jnp.float32
    )
    dspikes = jnp.einsum(
        "nkd,kcd->nc",
        grad_cols,
        weights.reshape(9, chans, chans),
        preferred_element_type=jnp.float32,
    )
    dspikes = dspikes.reshape(steps_count, samples, rows, cols, chans)
    carried = jnp.zeros((samples, rows, cols, chans), jnp.float32)
    outs = [None] * steps_count
    for position in reversed(range(steps_count)):
        carried = dspikes[position] * surrogate(potential_all[position]) + 0.5 * carried
        outs[position] = (cotangent[position].astype(jnp.float32) + carried).astype(jnp.bfloat16)
    grad_input = jnp.stack(outs)
    membrane_grad = 0.5 * carried
    total_cells = samples * data_count * lax.axis_size("rep") * rows * lax.axis_size("space") * cols
    names = [entry for axis in ("dp",) + rest for entry in reversed(bits_of(axis))]
    piece_shape = (weight_local.shape[0] // 2 ** len(names), weight_local.shape[1])
    blocks = lax.optimization_barrier(weight_local).reshape((2,) * len(names) + piece_shape)
    space_bits, rep_bits, dp_bits = bits_of("space"), bits_of("rep"), bits_of("dp")
    blocks, names = halving_scatter(blocks, names, space_bits[:1])
    half = chans // 2
    orders = (space_bits[1:] + rep_bits + dp_bits, rep_bits + space_bits[1:] + dp_bits)
    shard_part = jnp.concatenate(
        [
            halving_scatter(blocks[..., part * half : (part + 1) * half], names, order)[0]
            for part, order in enumerate(orders)
        ],
        axis=1,
    )
    summed = lax.all_gather(shard_part, rest, axis=0, tiled=True)
    weight_grad = summed * (1.0 / math.sqrt(steps_count * total_cells))
    new_moment = 0.9 * moment + 0.1 * weight_grad
    new_second = 0.95 * second + 0.05 * weight_grad * weight_grad
    update = new_moment / (jnp.sqrt(new_second) + 1e-08)
    return (grad_input, membrane_grad, weight_grad, new_moment, new_second, update)


def solution(mesh):
    return jax.shard_map(
        on_device,
        mesh=mesh,
        in_specs=(
            P(None, ("dp", "rep"), "space", None, None),
            P(("dp", "rep"), "space", None, None),
            P(None, ("dp", "rep"), "space", None, None),
            P("dp", None),
            P("dp", None),
            P("dp", None),
        ),
        out_specs=(
            P(None, ("dp", "rep"), "space", None, None),
            P(("dp", "rep"), "space", None, None),
            P("dp", None),
            P("dp", None),
            P("dp", None),
            P("dp", None),
        ),
        check_vma=False,
    )
```

```python
import math

import jax
import jax.numpy as jnp
from jax import lax
from jax.sharding import PartitionSpec as P


def extended(x, sides, width):
    for axis, dim in sides:
        peers, length = (lax.axis_size(axis), x.shape[dim])
        up = [(i, (i + 1) % peers) for i in range(peers - 1)]
        down = [(j, i) for i, j in up]
        last = lax.slice_in_dim(x, length - width, length, axis=dim)
        first = lax.slice_in_dim(x, 0, width, axis=dim)
        before = lax.ppermute(last, axis, up)
        after = lax.ppermute(first, axis, down)
        x = jnp.concatenate([before, x, after], axis=dim)
    return x


def doubling_gather(blocks, axis):
    peers = lax.axis_size(axis)
    me = lax.axis_index(axis)
    bit = 0
    while (1 << bit) < peers:
        pairs = [(j, j ^ (1 << bit)) for j in range(peers)]
        other = lax.ppermute(blocks, axis, pairs)
        low = (me // (1 << bit)) % 2 == 0
        blocks = jnp.where(low, jnp.concatenate([blocks, other]), jnp.concatenate([other, blocks]))
        bit += 1
    return blocks


def halving_scatter(blocks, names, stages):
    names = list(names)
    for axis, bit in stages:
        dim = names.index((axis, bit))
        peers = lax.axis_size(axis)
        first = (lax.axis_index(axis) // (1 << bit)) % 2 == 0
        low = lax.index_in_dim(blocks, 0, dim, keepdims=False)
        high = lax.index_in_dim(blocks, 1, dim, keepdims=False)
        pairs = [(j, j ^ (1 << bit)) for j in range(peers)]
        sent = lax.ppermute(jnp.where(first, high, low), axis, pairs)
        blocks = jnp.where(first, low, high) + sent
        names.pop(dim)
    return blocks, names


def bits_of(axis):
    return [(axis, bit) for bit in range(lax.axis_size(axis).bit_length() - 1)]


def surrogate(potential):
    return 1.0 / (1.0 + (math.pi * (potential - 1.0)) ** 2)


def offsets_list():
    return [(row_shift, col_shift) for row_shift in (-1, 0, 1) for col_shift in (-1, 0, 1)]


def on_device(frames, membrane, cotangent, master, moment, second):
    steps_count, samples, rows, cols, chans = frames.shape
    rest = ("space", "rep")
    rest_count = lax.axis_size("space") * lax.axis_size("rep")
    data_count = lax.axis_size("dp")
    shard_rows = master.shape[0]
    piece_rows = shard_rows // rest_count
    local = master.astype(jnp.bfloat16)
    piece = lax.dynamic_slice_in_dim(local, lax.axis_index(rest) * piece_rows, piece_rows, 0)
    weights = lax.all_gather(piece, ("dp",) + rest, axis=0, tiled=True)
    stacked = jnp.concatenate([membrane[None], frames], axis=0)
    rimmed = extended(stacked, (("space", 2),), 1)
    voltage = rimmed[0].astype(jnp.float32)
    potentials = []
    fired = []
    for position in range(steps_count):
        potential = 0.5 * voltage + rimmed[position + 1].astype(jnp.float32)
        spikes = jnp.where(potential >= 1.0, jnp.float32(1.0), jnp.float32(0.0))
        voltage = potential - spikes
        potentials.append(potential[:, 1:-1])
        fired.append(spikes)
    potential_all = jnp.stack(potentials)
    spike_all = jnp.stack(fired).astype(jnp.bfloat16)
    col_pad = ((0, 0), (0, 0), (0, 0), (1, 1), (0, 0))
    spike_pad = jnp.pad(spike_all, col_pad)
    grad_rim = extended(cotangent, (("space", 2),), 1)
    grad_pad = jnp.pad(grad_rim, col_pad)
    spike_cols = jnp.concatenate(
        [spike_pad[:, :, 1 + a : 1 + a + rows, 1 + b : 1 + b + cols] for a, b in offsets_list()],
        axis=-1,
    ).reshape(-1, 9 * chans)
    grad_cols = jnp.concatenate(
        [grad_pad[:, :, 1 - a : 1 - a + rows, 1 - b : 1 - b + cols] for a, b in offsets_list()],
        axis=-1,
    ).reshape(-1, 9, chans)
    grad_flat = cotangent.reshape(-1, chans)
    weight_local = lax.dot_general(
        spike_cols, grad_flat, (((0,), (0,)), ((), ())), preferred_element_type=jnp.float32
    )
    dspikes = jnp.einsum(
        "nkd,kcd->nc",
        grad_cols,
        weights.reshape(9, chans, chans),
        preferred_element_type=jnp.float32,
    )
    dspikes = dspikes.reshape(steps_count, samples, rows, cols, chans)
    carried = jnp.zeros((samples, rows, cols, chans), jnp.float32)
    outs = [None] * steps_count
    for position in reversed(range(steps_count)):
        carried = dspikes[position] * surrogate(potential_all[position]) + 0.5 * carried
        outs[position] = (cotangent[position].astype(jnp.float32) + carried).astype(jnp.bfloat16)
    grad_input = jnp.stack(outs)
    membrane_grad = 0.5 * carried
    total_cells = samples * data_count * lax.axis_size("rep") * rows * lax.axis_size("space") * cols
    names = [entry for axis in ("dp",) + rest for entry in reversed(bits_of(axis))]
    piece_shape = (weight_local.shape[0] // 2 ** len(names), weight_local.shape[1])
    space_bits, rep_bits, dp_bits = bits_of("space"), bits_of("rep"), bits_of("dp")
    place = names.index(space_bits[0])
    view = lax.optimization_barrier(weight_local).reshape(2**place, 2, -1, chans)
    first = lax.axis_index("space") % 2 == 0
    low, high = view[:, 0], view[:, 1]
    sent = lax.ppermute(jnp.where(first, high, low), "space", [(j, j ^ 1) for j in range(lax.axis_size("space"))])
    partial = jnp.where(first, low, high) + sent
    names.pop(place)
    blocks = partial.reshape((2,) * len(names) + piece_shape)
    half = chans // 2
    orders = (space_bits[1:] + rep_bits + dp_bits, rep_bits + space_bits[1:] + dp_bits)
    shard_part = jnp.concatenate(
        [
            halving_scatter(blocks[..., part * half : (part + 1) * half], names, order)[0]
            for part, order in enumerate(orders)
        ],
        axis=1,
    )
    summed = lax.all_gather(shard_part, rest, axis=0, tiled=True)
    weight_grad = summed * (1.0 / math.sqrt(steps_count * total_cells))
    new_moment = 0.9 * moment + 0.1 * weight_grad
    new_second = 0.95 * second + 0.05 * weight_grad * weight_grad
    update = new_moment / (jnp.sqrt(new_second) + 1e-08)
    return (grad_input, membrane_grad, weight_grad, new_moment, new_second, update)


def solution(mesh):
    return jax.shard_map(
        on_device,
        mesh=mesh,
        in_specs=(
            P(None, ("dp", "rep"), "space", None, None),
            P(("dp", "rep"), "space", None, None),
            P(None, ("dp", "rep"), "space", None, None),
            P("dp", None),
            P("dp", None),
            P("dp", None),
        ),
        out_specs=(
            P(None, ("dp", "rep"), "space", None, None),
            P(("dp", "rep"), "space", None, None),
            P("dp", None),
            P("dp", None),
            P("dp", None),
            P("dp", None),
        ),
        check_vma=False,
    )
```

```python
import math

import jax
import jax.numpy as jnp
from jax import lax
from jax.sharding import PartitionSpec as P


def extended(x, sides, width):
    for axis, dim in sides:
        peers, length = (lax.axis_size(axis), x.shape[dim])
        up = [(i, (i + 1) % peers) for i in range(peers - 1)]
        down = [(j, i) for i, j in up]
        last = lax.slice_in_dim(x, length - width, length, axis=dim)
        first = lax.slice_in_dim(x, 0, width, axis=dim)
        before = lax.ppermute(last, axis, up)
        after = lax.ppermute(first, axis, down)
        x = jnp.concatenate([before, x, after], axis=dim)
    return x


def doubling_gather(blocks, axis):
    peers = lax.axis_size(axis)
    me = lax.axis_index(axis)
    bit = 0
    while (1 << bit) < peers:
        pairs = [(j, j ^ (1 << bit)) for j in range(peers)]
        other = lax.ppermute(blocks, axis, pairs)
        low = (me // (1 << bit)) % 2 == 0
        blocks = jnp.where(low, jnp.concatenate([blocks, other]), jnp.concatenate([other, blocks]))
        bit += 1
    return blocks


def halving_scatter(blocks, names, stages):
    names = list(names)
    for axis, bit in stages:
        dim = names.index((axis, bit))
        peers = lax.axis_size(axis)
        first = (lax.axis_index(axis) // (1 << bit)) % 2 == 0
        low = lax.index_in_dim(blocks, 0, dim, keepdims=False)
        high = lax.index_in_dim(blocks, 1, dim, keepdims=False)
        pairs = [(j, j ^ (1 << bit)) for j in range(peers)]
        sent = lax.ppermute(jnp.where(first, high, low), axis, pairs)
        blocks = jnp.where(first, low, high) + sent
        names.pop(dim)
    return blocks, names


def bits_of(axis):
    return [(axis, bit) for bit in range(lax.axis_size(axis).bit_length() - 1)]


def staged_gather(blocks, stages):
    for axis, bit in stages:
        peers = lax.axis_size(axis)
        pairs = [(j, j ^ (1 << bit)) for j in range(peers)]
        other = lax.ppermute(blocks, axis, pairs)
        low = (lax.axis_index(axis) // (1 << bit)) % 2 == 0
        blocks = jnp.where(low, jnp.stack([blocks, other]), jnp.stack([other, blocks]))
    return blocks


def rest_gather(blocks, axes):
    natural = [(axis, bit) for axis in axes for bit in reversed(range(lax.axis_size(axis).bit_length() - 1))]
    stages = natural[::-1]
    stages = [e for e in stages if e[0] != "space"] + [e for e in natural if e[0] == "space"]
    gathered = staged_gather(blocks, stages)
    held = stages[::-1]
    order = [held.index(entry) for entry in natural]
    gathered = jnp.transpose(gathered, order + list(range(len(stages), gathered.ndim)))
    return gathered.reshape((2 ** len(stages),) + blocks.shape)


def surrogate(potential):
    return 1.0 / (1.0 + (math.pi * (potential - 1.0)) ** 2)


def offsets_list():
    return [(row_shift, col_shift) for row_shift in (-1, 0, 1) for col_shift in (-1, 0, 1)]


def on_device(frames, membrane, cotangent, master, moment, second):
    steps_count, samples, rows, cols, chans = frames.shape
    rest = ("space", "rep")
    rest_count = lax.axis_size("space") * lax.axis_size("rep")
    data_count = lax.axis_size("dp")
    shard_rows = master.shape[0]
    piece_rows = shard_rows // rest_count
    local = master.astype(jnp.bfloat16)
    piece = lax.dynamic_slice_in_dim(local, lax.axis_index(rest) * piece_rows, piece_rows, 0)
    weights = lax.all_gather(piece, ("dp",) + rest, axis=0, tiled=True)
    stacked = jnp.concatenate([membrane[None], frames], axis=0)
    rimmed = extended(stacked, (("space", 2),), 1)
    voltage = rimmed[0].astype(jnp.float32)
    potentials = []
    fired = []
    for position in range(steps_count):
        potential = 0.5 * voltage + rimmed[position + 1].astype(jnp.float32)
        spikes = jnp.where(potential >= 1.0, jnp.float32(1.0), jnp.float32(0.0))
        voltage = potential - spikes
        potentials.append(potential[:, 1:-1])
        fired.append(spikes)
    potential_all = jnp.stack(potentials)
    spike_all = jnp.stack(fired).astype(jnp.bfloat16)
    col_pad = ((0, 0), (0, 0), (0, 0), (1, 1), (0, 0))
    spike_pad = jnp.pad(spike_all, col_pad)
    grad_rim = extended(cotangent, (("space", 2),), 1)
    grad_pad = jnp.pad(grad_rim, col_pad)
    spike_cols = jnp.concatenate(
        [spike_pad[:, :, 1 + a : 1 + a + rows, 1 + b : 1 + b + cols] for a, b in offsets_list()],
        axis=-1,
    ).reshape(-1, 9 * chans)
    grad_cols = jnp.concatenate(
        [grad_pad[:, :, 1 - a : 1 - a + rows, 1 - b : 1 - b + cols] for a, b in offsets_list()],
        axis=-1,
    ).reshape(-1, 9, chans)
    grad_flat = cotangent.reshape(-1, chans)
    weight_local = lax.dot_general(
        spike_cols, grad_flat, (((0,), (0,)), ((), ())), preferred_element_type=jnp.float32
    )
    dspikes = jnp.einsum(
        "nkd,kcd->nc",
        grad_cols,
        weights.reshape(9, chans, chans),
        preferred_element_type=jnp.float32,
    )
    dspikes = dspikes.reshape(steps_count, samples, rows, cols, chans)
    carried = jnp.zeros((samples, rows, cols, chans), jnp.float32)
    outs = [None] * steps_count
    for position in reversed(range(steps_count)):
        carried = dspikes[position] * surrogate(potential_all[position]) + 0.5 * carried
        outs[position] = (cotangent[position].astype(jnp.float32) + carried).astype(jnp.bfloat16)
    grad_input = jnp.stack(outs)
    membrane_grad = 0.5 * carried
    total_cells = samples * data_count * lax.axis_size("rep") * rows * lax.axis_size("space") * cols
    names = [entry for axis in ("dp",) + rest for entry in reversed(bits_of(axis))]
    piece_shape = (weight_local.shape[0] // 2 ** len(names), weight_local.shape[1])
    blocks = lax.optimization_barrier(weight_local).reshape((2,) * len(names) + piece_shape)
    space_bits, rep_bits, dp_bits = bits_of("space"), bits_of("rep"), bits_of("dp")
    blocks, names = halving_scatter(blocks, names, space_bits[:1])
    half = chans // 2
    orders = (space_bits[1:] + rep_bits + dp_bits, rep_bits + space_bits[1:] + dp_bits)
    shard_part = jnp.concatenate(
        [
            halving_scatter(blocks[..., part * half : (part + 1) * half], names, order)[0]
            for part, order in enumerate(orders)
        ],
        axis=1,
    )
    summed = rest_gather(shard_part, rest).reshape(-1, chans)
    weight_grad = summed * (1.0 / math.sqrt(steps_count * total_cells))
    new_moment = 0.9 * moment + 0.1 * weight_grad
    new_second = 0.95 * second + 0.05 * weight_grad * weight_grad
    update = new_moment / (jnp.sqrt(new_second) + 1e-08)
    return (grad_input, membrane_grad, weight_grad, new_moment, new_second, update)


def solution(mesh):
    return jax.shard_map(
        on_device,
        mesh=mesh,
        in_specs=(
            P(None, ("dp", "rep"), "space", None, None),
            P(("dp", "rep"), "space", None, None),
            P(None, ("dp", "rep"), "space", None, None),
            P("dp", None),
            P("dp", None),
            P("dp", None),
        ),
        out_specs=(
            P(None, ("dp", "rep"), "space", None, None),
            P(("dp", "rep"), "space", None, None),
            P("dp", None),
            P("dp", None),
            P("dp", None),
            P("dp", None),
        ),
        check_vma=False,
    )
```

```python
import math

import jax
import jax.numpy as jnp
from jax import lax
from jax.sharding import PartitionSpec as P


def extended(x, sides, width):
    for axis, dim in sides:
        peers, length = (lax.axis_size(axis), x.shape[dim])
        up = [(i, (i + 1) % peers) for i in range(peers - 1)]
        down = [(j, i) for i, j in up]
        last = lax.slice_in_dim(x, length - width, length, axis=dim)
        first = lax.slice_in_dim(x, 0, width, axis=dim)
        before = lax.ppermute(last, axis, up)
        after = lax.ppermute(first, axis, down)
        x = jnp.concatenate([before, x, after], axis=dim)
    return x


def doubling_gather(blocks, axis):
    peers = lax.axis_size(axis)
    me = lax.axis_index(axis)
    bit = 0
    while (1 << bit) < peers:
        pairs = [(j, j ^ (1 << bit)) for j in range(peers)]
        other = lax.ppermute(blocks, axis, pairs)
        low = (me // (1 << bit)) % 2 == 0
        blocks = jnp.where(low, jnp.concatenate([blocks, other]), jnp.concatenate([other, blocks]))
        bit += 1
    return blocks


def halving_scatter(blocks, names, stages):
    names = list(names)
    for axis, bit in stages:
        dim = names.index((axis, bit))
        peers = lax.axis_size(axis)
        first = (lax.axis_index(axis) // (1 << bit)) % 2 == 0
        low = lax.index_in_dim(blocks, 0, dim, keepdims=False)
        high = lax.index_in_dim(blocks, 1, dim, keepdims=False)
        pairs = [(j, j ^ (1 << bit)) for j in range(peers)]
        sent = lax.ppermute(jnp.where(first, high, low), axis, pairs)
        blocks = jnp.where(first, low, high) + sent
        names.pop(dim)
    return blocks, names


def bits_of(axis):
    return [(axis, bit) for bit in range(lax.axis_size(axis).bit_length() - 1)]


def surrogate(potential):
    return 1.0 / (1.0 + (math.pi * (potential - 1.0)) ** 2)


def offsets_list():
    return [(row_shift, col_shift) for row_shift in (-1, 0, 1) for col_shift in (-1, 0, 1)]


def on_device(frames, membrane, cotangent, master, moment, second):
    steps_count, samples, rows, cols, chans = frames.shape
    rest = ("space", "rep")
    rest_count = lax.axis_size("space") * lax.axis_size("rep")
    data_count = lax.axis_size("dp")
    shard_rows = master.shape[0]
    piece_rows = shard_rows // rest_count
    local = master.astype(jnp.bfloat16)
    piece = lax.dynamic_slice_in_dim(local, lax.axis_index(rest) * piece_rows, piece_rows, 0)
    weights = lax.all_gather(piece, ("dp",) + rest, axis=0, tiled=True)
    stacked = jnp.concatenate([membrane[None], frames], axis=0)
    rimmed = extended(stacked, (("space", 2),), 1)
    voltage = rimmed[0].astype(jnp.float32)
    potentials = []
    fired = []
    for position in range(steps_count):
        potential = 0.5 * voltage + rimmed[position + 1].astype(jnp.float32)
        spikes = jnp.where(potential >= 1.0, jnp.float32(1.0), jnp.float32(0.0))
        voltage = potential - spikes
        potentials.append(potential[:, 1:-1])
        fired.append(spikes)
    potential_all = jnp.stack(potentials)
    spike_all = jnp.stack(fired).astype(jnp.bfloat16)
    col_pad = ((0, 0), (0, 0), (0, 0), (1, 1), (0, 0))
    spike_pad = jnp.pad(spike_all, col_pad)
    grad_rim = extended(cotangent, (("space", 2),), 1)
    grad_pad = jnp.pad(grad_rim, col_pad)
    spike_cols = jnp.concatenate(
        [spike_pad[:, :, 1 + a : 1 + a + rows, 1 + b : 1 + b + cols] for a, b in offsets_list()],
        axis=-1,
    ).reshape(-1, 9 * chans)
    grad_cols = jnp.concatenate(
        [grad_pad[:, :, 1 - a : 1 - a + rows, 1 - b : 1 - b + cols] for a, b in offsets_list()],
        axis=-1,
    ).reshape(-1, 9, chans)
    grad_flat = cotangent.reshape(-1, chans)
    half = chans // 2
    weight_halves = [
        lax.dot_general(
            spike_cols, grad_flat[:, part * half : (part + 1) * half], (((0,), (0,)), ((), ())),
            preferred_element_type=jnp.float32,
        )
        for part in range(2)
    ]
    dspikes = jnp.einsum(
        "nkd,kcd->nc",
        grad_cols,
        weights.reshape(9, chans, chans),
        preferred_element_type=jnp.float32,
    )
    dspikes = dspikes.reshape(steps_count, samples, rows, cols, chans)
    carried = jnp.zeros((samples, rows, cols, chans), jnp.float32)
    outs = [None] * steps_count
    for position in reversed(range(steps_count)):
        carried = dspikes[position] * surrogate(potential_all[position]) + 0.5 * carried
        outs[position] = (cotangent[position].astype(jnp.float32) + carried).astype(jnp.bfloat16)
    grad_input = jnp.stack(outs)
    membrane_grad = 0.5 * carried
    total_cells = samples * data_count * lax.axis_size("rep") * rows * lax.axis_size("space") * cols
    names = [entry for axis in ("dp",) + rest for entry in reversed(bits_of(axis))]
    piece_shape = (weight_halves[0].shape[0] // 2 ** len(names), half)
    space_bits, rep_bits, dp_bits = bits_of("space"), bits_of("rep"), bits_of("dp")
    orders = (space_bits + rep_bits + dp_bits, space_bits[:1] + rep_bits + space_bits[1:] + dp_bits)
    shard_part = jnp.concatenate(
        [
            halving_scatter(
                lax.optimization_barrier(part).reshape((2,) * len(names) + piece_shape), names, order
            )[0]
            for part, order in zip(weight_halves, orders)
        ],
        axis=1,
    )
    summed = lax.all_gather(shard_part, rest, axis=0, tiled=True)
    weight_grad = summed * (1.0 / math.sqrt(steps_count * total_cells))
    new_moment = 0.9 * moment + 0.1 * weight_grad
    new_second = 0.95 * second + 0.05 * weight_grad * weight_grad
    update = new_moment / (jnp.sqrt(new_second) + 1e-08)
    return (grad_input, membrane_grad, weight_grad, new_moment, new_second, update)


def solution(mesh):
    return jax.shard_map(
        on_device,
        mesh=mesh,
        in_specs=(
            P(None, ("dp", "rep"), "space", None, None),
            P(("dp", "rep"), "space", None, None),
            P(None, ("dp", "rep"), "space", None, None),
            P("dp", None),
            P("dp", None),
            P("dp", None),
        ),
        out_specs=(
            P(None, ("dp", "rep"), "space", None, None),
            P(("dp", "rep"), "space", None, None),
            P("dp", None),
            P("dp", None),
            P("dp", None),
            P("dp", None),
        ),
        check_vma=False,
    )
```

```python
import math

import jax
import jax.numpy as jnp
from jax import lax
from jax.sharding import PartitionSpec as P


def extended(x, sides, width):
    for axis, dim in sides:
        peers, length = (lax.axis_size(axis), x.shape[dim])
        up = [(i, (i + 1) % peers) for i in range(peers - 1)]
        down = [(j, i) for i, j in up]
        last = lax.slice_in_dim(x, length - width, length, axis=dim)
        first = lax.slice_in_dim(x, 0, width, axis=dim)
        before = lax.ppermute(last, axis, up)
        after = lax.ppermute(first, axis, down)
        x = jnp.concatenate([before, x, after], axis=dim)
    return x


def doubling_gather(blocks, axis):
    peers = lax.axis_size(axis)
    me = lax.axis_index(axis)
    bit = 0
    while (1 << bit) < peers:
        pairs = [(j, j ^ (1 << bit)) for j in range(peers)]
        other = lax.ppermute(blocks, axis, pairs)
        low = (me // (1 << bit)) % 2 == 0
        blocks = jnp.where(low, jnp.concatenate([blocks, other]), jnp.concatenate([other, blocks]))
        bit += 1
    return blocks


def halving_scatter(blocks, names, stages):
    names = list(names)
    for axis, bit in stages:
        dim = names.index((axis, bit))
        peers = lax.axis_size(axis)
        first = (lax.axis_index(axis) // (1 << bit)) % 2 == 0
        low = lax.index_in_dim(blocks, 0, dim, keepdims=False)
        high = lax.index_in_dim(blocks, 1, dim, keepdims=False)
        pairs = [(j, j ^ (1 << bit)) for j in range(peers)]
        sent = lax.ppermute(jnp.where(first, high, low), axis, pairs)
        blocks = jnp.where(first, low, high) + sent
        names.pop(dim)
    return blocks, names


def bits_of(axis):
    return [(axis, bit) for bit in range(lax.axis_size(axis).bit_length() - 1)]


def surrogate(potential):
    return 1.0 / (1.0 + (math.pi * (potential - 1.0)) ** 2)


def offsets_list():
    return [(row_shift, col_shift) for row_shift in (-1, 0, 1) for col_shift in (-1, 0, 1)]


def on_device(frames, membrane, cotangent, master, moment, second):
    steps_count, samples, rows, cols, chans = frames.shape
    rest = ("space", "rep")
    rest_count = lax.axis_size("space") * lax.axis_size("rep")
    data_count = lax.axis_size("dp")
    shard_rows = master.shape[0]
    piece_rows = shard_rows // rest_count
    local = master.astype(jnp.bfloat16)
    piece = lax.dynamic_slice_in_dim(local, lax.axis_index(rest) * piece_rows, piece_rows, 0)
    weights = lax.all_gather(piece, ("dp",) + rest, axis=0, tiled=True)
    stacked = jnp.concatenate([membrane[None], frames], axis=0)
    rimmed = extended(stacked, (("space", 2),), 1)
    voltage = rimmed[0].astype(jnp.float32)
    potentials = []
    fired = []
    for position in range(steps_count):
        potential = 0.5 * voltage + rimmed[position + 1].astype(jnp.float32)
        spikes = jnp.where(potential >= 1.0, jnp.float32(1.0), jnp.float32(0.0))
        voltage = potential - spikes
        potentials.append(potential[:, 1:-1])
        fired.append(spikes)
    potential_all = jnp.stack(potentials)
    spike_all = jnp.stack(fired).astype(jnp.bfloat16)
    col_pad = ((0, 0), (0, 0), (0, 0), (1, 1), (0, 0))
    spike_pad = jnp.pad(spike_all, col_pad)
    grad_rim = extended(cotangent, (("space", 2),), 1)
    grad_pad = jnp.pad(grad_rim, col_pad)
    spike_cols = jnp.concatenate(
        [spike_pad[:, :, 1 + a : 1 + a + rows, 1 + b : 1 + b + cols] for a, b in offsets_list()],
        axis=-1,
    ).reshape(-1, 9 * chans)
    grad_cols = jnp.concatenate(
        [grad_pad[:, :, 1 - a : 1 - a + rows, 1 - b : 1 - b + cols] for a, b in offsets_list()],
        axis=-1,
    ).reshape(-1, 9, chans)
    grad_flat = cotangent.reshape(-1, chans)
    weight_local = lax.dot_general(
        spike_cols, grad_flat, (((0,), (0,)), ((), ())), preferred_element_type=jnp.float32
    )
    dspikes = jnp.einsum(
        "nkd,kcd->nc",
        grad_cols,
        weights.reshape(9, chans, chans),
        preferred_element_type=jnp.float32,
    )
    dspikes = dspikes.reshape(steps_count, samples, rows, cols, chans)
    carried = jnp.zeros((samples, rows, cols, chans), jnp.float32)
    outs = [None] * steps_count
    for position in reversed(range(steps_count)):
        carried = dspikes[position] * surrogate(potential_all[position]) + 0.5 * carried
        outs[position] = (cotangent[position].astype(jnp.float32) + carried).astype(jnp.bfloat16)
    grad_input = jnp.stack(outs)
    membrane_grad = 0.5 * carried
    total_cells = samples * data_count * lax.axis_size("rep") * rows * lax.axis_size("space") * cols
    names = [entry for axis in ("dp",) + rest for entry in reversed(bits_of(axis))]
    piece_shape = (weight_local.shape[0] // 2 ** len(names), weight_local.shape[1])
    blocks = lax.optimization_barrier(weight_local).reshape((2,) * len(names) + piece_shape)
    space_bits, rep_bits, dp_bits = bits_of("space"), bits_of("rep"), bits_of("dp")
    blocks, names = halving_scatter(blocks, names, space_bits[:1])
    half = chans // 2
    orders = (space_bits[1:] + rep_bits + dp_bits, rep_bits + dp_bits[:1] + space_bits[1:] + dp_bits[1:])
    shard_part = jnp.concatenate(
        [
            halving_scatter(blocks[..., part * half : (part + 1) * half], names, order)[0]
            for part, order in enumerate(orders)
        ],
        axis=1,
    )
    summed = lax.all_gather(shard_part, rest, axis=0, tiled=True)
    weight_grad = summed * (1.0 / math.sqrt(steps_count * total_cells))
    new_moment = 0.9 * moment + 0.1 * weight_grad
    new_second = 0.95 * second + 0.05 * weight_grad * weight_grad
    update = new_moment / (jnp.sqrt(new_second) + 1e-08)
    return (grad_input, membrane_grad, weight_grad, new_moment, new_second, update)


def solution(mesh):
    return jax.shard_map(
        on_device,
        mesh=mesh,
        in_specs=(
            P(None, ("dp", "rep"), "space", None, None),
            P(("dp", "rep"), "space", None, None),
            P(None, ("dp", "rep"), "space", None, None),
            P("dp", None),
            P("dp", None),
            P("dp", None),
        ),
        out_specs=(
            P(None, ("dp", "rep"), "space", None, None),
            P(("dp", "rep"), "space", None, None),
            P("dp", None),
            P("dp", None),
            P("dp", None),
            P("dp", None),
        ),
        check_vma=False,
    )
```
